32 devices in a mesh: dp: 8 (over z, x), expert: 4 (over y, core).
Axes of the slice: x: 2, y: 2, z: 4, core: 2. Of those that a mesh axis runs over, the one named last changes fastest.
Arguments:
- hidden: bfloat16 [2048, 2304], P(('dp', 'expert')), may hold values from -6 to 6
- tree_qkv: bfloat16 [2048, 6912], P(('dp', 'expert')), may hold values from -7 to 7
- prompt_kv: bfloat16 [8, 512, 4608], P('dp', 'expert'), may hold values from -6 to 6
- prompt_len: int32 [8], P('dp'), may hold values from 128 to 512, as said below
- private_kv: bfloat16 [32, 512, 4608], P(('dp', 'expert')), may hold values from -6 to 6
- priv_len: int32 [32], P(('dp', 'expert')), may hold values from 1 to 512, as said below
- parents: int32 [32, 64], P(('dp', 'expert')), may hold values from -1 to 62, as said below
- leaf: int32 [32], P(('dp', 'expert')), may hold values from 0 to 63
- w_out: bfloat16 [2304, 2304], replicated, may hold values from -3 to 3
- norm_gain: float32 [2304], replicated, may hold values from 0.1 to 1.9
- w_router: bfloat16 [2304, 4], replicated, as said below
- routes: int32 [2048, 2], P(('dp', 'expert')), may hold values from 0 to 3, all different within a row; in each aligned block of 64 rows (0 to 63, 64 to 127, ...) at most 48 rows name the same one
- w_gate_up: bfloat16 [4, 2, 2304, 5760], P('expert', None, None, 'dp'), may hold values from -0.125 to 0.125
- w_down: bfloat16 [4, 5760, 2304], P('expert', 'dp'), may hold values from -0.15625 to 0.15625
Outputs:
- layer_out: bfloat16 [2048, 2304], P(('dp', 'expert'))
- accepted_kv: bfloat16 [32, 64, 4608], P(('dp', 'expert'))
The draws below stay inside these ranges and needn't reach their ends.
Inputs may be any that keep to these rules, and one draw needn't show every extreme that they name: `routes`: the rows of one device (aligned blocks of 64 rows) name each expert at most 48 times; the two experts of a row differ. `prompt_len`: some group's length is exactly 512. `priv_len`: some request's length is exactly 512. parents[r, 0] = -1; for t >= 1, max(0, t - 8) <= parents[r, t] <= t - 1. `w_router`: entries lie within 3 / sqrt(27648) of zero.
All inputs are finite; a program needn't handle non-finite values.
Results may differ from the reference program's by a relative error of at most 0.014.
Values may be sent and summed in bfloat16 or wider, within the bound.
No kernel may reach another device: no remote copies, remote signals or barrier semaphores. Data moves between devices by JAX's collectives and lax.ppermute only.
A program may use at most 128 MiB of HBM per device.

```python
import math
import jax
import jax.numpy as jnp
import numpy as np
from jax import lax

D = 2304
H = 36
HD = 64
FF = 5760
TREE = 64
REQ_DEV = 1
PRIV = 512
EXPERTS = 4
GROUPS = 8
REQUESTS = 32
TOKENS = 2048
PROMPT = 512
CAP = 48
N_DP = 8


def rough_rows(key, count, features):
    return jnp.clip(jax.random.normal(jax.random.fold_in(key, 5), (count, features), jnp.float32), -6.0, 6.0)


def draw_tree_qkv(key, part):
    drawn = rough_rows(jax.random.fold_in(key, 31), TOKENS, 3 * D)
    return drawn.astype(jnp.bfloat16)


def draw_prompt_kv(key, part):
    drawn = rough_rows(jax.random.fold_in(key, 41), GROUPS * PROMPT, 2 * D).reshape(GROUPS, PROMPT, 2 * D)
    return drawn.astype(jnp.bfloat16)


def draw_prompt_len(key, part):
    lengths = jax.random.randint(jax.random.fold_in(key, 21), (GROUPS,), PROMPT // 4, PROMPT + 1)
    longest = jax.random.randint(jax.random.fold_in(key, 22), (), 0, GROUPS)
    return jnp.where(jnp.arange(GROUPS, dtype=jnp.int32) == longest, PROMPT, lengths).astype(jnp.int32)


def draw_priv_len(key, part):
    lengths = jax.random.randint(jax.random.fold_in(key, 23), (REQUESTS,), 1, PRIV + 1)
    longest = jax.random.randint(jax.random.fold_in(key, 24), (), 0, REQUESTS)
    return jnp.where(jnp.arange(REQUESTS, dtype=jnp.int32) == longest, PRIV, lengths).astype(jnp.int32)


def draw_parents(key, part):
    positions = jnp.arange(TREE, dtype=jnp.int32)
    lowest = jnp.maximum(positions - 8, 0)
    highest = jnp.maximum(positions, 1)
    chosen = jax.random.randint(jax.random.fold_in(key, 25), (REQUESTS, TREE), lowest[None, :], highest[None, :])
    return jnp.where(positions[None, :] == 0, -1, chosen).astype(jnp.int32)


def draw_w_router(key, part):
    spread = 1.0 / math.sqrt(12.0 * D)
    drawn = jnp.clip(jax.random.normal(jax.random.fold_in(key, 52), (D, EXPERTS), jnp.float32), -3.0, 3.0) * spread
    return drawn.astype(jnp.bfloat16)


def touch_ends(entries, rng, least, high):
    dims = entries.shape
    place = [jax.random.randint(jax.random.fold_in(rng, axis), (), 0, dims[axis]) for axis in range(len(dims))]
    entries = entries.at[tuple(place)].set(least)
    longest = dims.index(max(dims))
    place[longest] = (place[longest] + 1) % dims[longest]
    return entries.at[tuple(place)].set(high)


def steps_of(stream_key, dims, cuts, smallest, high):
    loudness, own = 1.0, jax.random.fold_in(stream_key, 6)
    for axis_at, shards_of in cuts:
        steps = jnp.exp(jax.random.uniform(jax.random.fold_in(own, axis_at), (shards_of,), jnp.float32, smallest / len(cuts), high / len(cuts)))
        loudness = loudness * jnp.repeat(steps, dims[axis_at] // shards_of).reshape([-1 if axis == axis_at else 1 for axis in range(len(dims))])
    return loudness


def shared_out(own_key, own, number, rows, number_of, top, reach, skew):
    order = jax.random.permutation(own_key, number_of)
    packed, usual = load_shares(number_of, rows * top, reach, skew, True), load_shares(number_of, rows * top, reach, skew, False)
    places = jnp.arange(number_of)

    def named(sizes, offset_by):
        used = int((sizes > 0).sum())
        fixed = max(1, used // 4)
        shifted = fixed + (places - fixed + offset_by * (used - fixed)) % max(1, number_of - fixed)
        return jnp.zeros((number_of,), jnp.int32).at[order[jnp.where(places < fixed, places, shifted)]].set(jnp.asarray(sizes, jnp.int32))

    sizes = jnp.where(number % 4 == 0, named(packed, number // 4), named(usual, number - number // 4 - 1))
    mixed = jax.random.permutation(jax.random.fold_in(own, 3), number_of)
    source_of, receiver = mixed[0:number_of // 2 * 2:2], mixed[1:number_of // 2 * 2:2]
    room = jnp.minimum(sizes[source_of] - 1, reach - sizes[receiver]) // 2
    room = jnp.where((source_of == order[0]) | (receiver == order[0]) | (sizes[receiver] == 0), 0, jnp.maximum(room, 0))
    shifted = jax.random.randint(jax.random.fold_in(own, 4), (number_of // 2,), 0, 1 << 20) % (room + 1)
    sizes = sizes.at[source_of].add(-shifted).at[receiver].add(shifted)
    labels = jnp.searchsorted(jnp.cumsum(sizes), jnp.arange(rows * top), side="right").astype(jnp.int32)
    listing = labels.reshape(top, rows).T
    listing = listing[jax.random.permutation(jax.random.fold_in(own, 1), rows)]
    offset_by = jax.random.randint(jax.random.fold_in(own, 2), (rows, 1), 0, top)
    return jnp.take_along_axis(listing, (jnp.arange(top)[None, :] + offset_by) % top, axis=1)


def load_shares(count, total, limit, skew, full):
    weights = [(1 << 20) // math.isqrt(rank ** skew) + 1 for rank in range(1, count + 1)]
    largest = limit if full else min(limit, max(-(-total // count), total * weights[0] // sum(weights)))
    least = 1 if total - largest >= count - 1 else 0
    counts, rest = [largest] + [least] * (count - 1), total - largest - least * (count - 1)
    while rest > 0:
        candidates = [i for i in range(1, count) if counts[i] < largest] or [i for i in range(1, count) if counts[i] < limit]
        pool, budget = sum([weights[i] for i in candidates]), rest
        for i in candidates:
            addition = min(limit - counts[i], max(1, budget * weights[i] // pool), rest)
            counts[i] = counts[i] + addition
            rest = rest - addition
    return np.array(counts)


def gaussian(stream_key, dims, scale, most, split=(), held_as=jnp.bfloat16):
    level = steps_of(stream_key, dims, split, -0.22, 0.18) if split else 1.0
    values = jax.random.normal(stream_key, dims, jnp.float32) * scale * level
    return jnp.minimum(jnp.maximum(values, -most), most).astype(held_as)


def setup_inputs(seed: int = 0) -> dict:
    key_of = jax.random.split(jax.random.key(seed), 15)
    hidden = gaussian(key_of[0], (TOKENS, D), 1.0, 6.0, ((0, 32),))
    tree_qkv = draw_tree_qkv(jax.random.fold_in(key_of[14], 71), 0)
    prompt_kv = draw_prompt_kv(jax.random.fold_in(key_of[14], 71), 0)
    prompt_len = draw_prompt_len(jax.random.fold_in(key_of[14], 71), 0)
    private_kv = gaussian(key_of[4], (REQUESTS, PRIV, 2 * D), 1.0, 6.0, ((0, 32),))
    priv_len = draw_priv_len(jax.random.fold_in(key_of[14], 71), 0)
    parents = draw_parents(jax.random.fold_in(key_of[14], 71), 0)
    leaf = touch_ends(jax.random.randint(key_of[7], (REQUESTS,), 0, TREE), jax.random.fold_in(key_of[7], 1), 0, TREE - 1).astype(jnp.int32)
    w_out = gaussian(key_of[8], (D, D), (max(D // 512, 1)) ** -0.5, 3.0)
    norm_gain = jnp.clip(1.0 + 0.18 * jax.random.normal(key_of[9], (D,), jnp.float32), 0.1, 1.9)
    w_router = draw_w_router(jax.random.fold_in(key_of[14], 71), 0)
    routes_keys = jax.random.split(jax.random.fold_in(key_of[11], 1), TOKENS // (REQ_DEV * TREE))
    routes_turns = jax.random.permutation(jax.random.fold_in(key_of[11], 3), TOKENS // (REQ_DEV * TREE))
    routes = jax.vmap(lambda own, number: shared_out(jax.random.fold_in(key_of[11], 2), own, number, REQ_DEV * TREE, EXPERTS, 2, CAP, 2))(routes_keys, routes_turns).reshape((TOKENS, 2))
    w_gate_up = gaussian(key_of[12], (EXPERTS, 2, D, FF), D ** -0.5, 0.125, ((0, 4), (3, 8)))
    w_down = gaussian(key_of[13], (EXPERTS, FF, D), (FF // 4) ** -0.5, 0.15625, ((0, 4), (1, 8)))
    return dict(hidden=hidden, tree_qkv=tree_qkv, prompt_kv=prompt_kv, prompt_len=prompt_len, private_kv=private_kv, priv_len=priv_len, parents=parents, leaf=leaf, w_out=w_out, norm_gain=norm_gain, w_router=w_router, routes=routes, w_gate_up=w_gate_up, w_down=w_down)


NEG = -1e+30
EPS = 1e-05
HIGH = lax.Precision.HIGHEST

def closure(parents):
    count = parents.shape[-1]
    columns = jnp.arange(count, dtype=jnp.int32)
    reached = (parents[:, :, None] == columns[None, None, :]).astype(jnp.float32) + jnp.eye(count, dtype=jnp.float32)[None]
    for sweeps in range((count - 1).bit_length()):
        reached = jnp.minimum(jnp.einsum('rij,rjk->rik', reached, reached, precision=HIGH), 1.0)
    return reached

def compact(reach_one, leaf_one, kv_one):
    count = reach_one.shape[0]
    marked = lax.optimization_barrier(jnp.sum(jnp.where(jnp.arange(count, dtype=jnp.int32)[:, None] == leaf_one, reach_one, 0.0), axis=0))
    earlier = (jnp.arange(count, dtype=jnp.int32)[None, :] < jnp.arange(count, dtype=jnp.int32)[:, None]).astype(jnp.float32)
    ordinal = jnp.dot(earlier, marked, precision=HIGH)
    slot_ids = jnp.arange(count, dtype=jnp.int32).astype(jnp.float32)
    chosen = jnp.where(slot_ids[:, None] == ordinal[None, :], marked[None, :], 0.0)
    return jnp.dot(chosen.astype(jnp.bfloat16), kv_one, preferred_element_type=jnp.float32).astype(jnp.bfloat16)

def one_request(request_id, qkv_rows, private_rows, private_len, parent_rows, leaf_one, prompt_kv, prompt_len):
    group_id = request_id // (REQUESTS // GROUPS)
    prompt_rows = lax.dynamic_index_in_dim(prompt_kv, group_id, 0, keepdims=False)
    prompt_limit = lax.dynamic_index_in_dim(prompt_len, group_id, 0, keepdims=False)
    query_vectors = qkv_rows[:, :D].reshape(TREE, H, HD).astype(jnp.float32)
    new_kv = qkv_rows[:, D:]
    cache_rows = jnp.concatenate([prompt_rows, private_rows, new_kv], axis=0)
    reached = closure(parent_rows[None])[0]
    prompt_ok = jnp.broadcast_to((jnp.arange(PROMPT, dtype=jnp.int32) < prompt_limit)[None, :], (TREE, PROMPT))
    private_ok = jnp.broadcast_to((jnp.arange(PRIV, dtype=jnp.int32) < private_len)[None, :], (TREE, PRIV))
    allowed = jnp.concatenate([prompt_ok, private_ok, reached > 0.5], axis=1)
    key_matrix_rows = cache_rows[:, :D].reshape(-1, H, HD).astype(jnp.float32)
    value_matrix_rows = cache_rows[:, D:].reshape(-1, H, HD).astype(jnp.float32)
    attention_score_scale = 1.0 / math.sqrt(HD)
    attention_scores = jnp.einsum('jec,oec->jeo', query_vectors, key_matrix_rows) * attention_score_scale
    attention_scores = jnp.where(allowed[:, None, :], attention_scores, NEG)
    highest = lax.optimization_barrier(jnp.max(attention_scores, axis=-1, keepdims=True))
    attention_weights = jnp.where(allowed[:, None, :], jnp.exp(attention_scores - highest), 0.0)
    totals = lax.optimization_barrier(jnp.sum(attention_weights, axis=-1))
    rounded_result = attention_weights.astype(jnp.bfloat16).astype(jnp.float32)
    weighted_sum = jnp.einsum('fxy,yxv->fxv', rounded_result, value_matrix_rows)
    context = (weighted_sum / totals[..., None]).reshape(TREE, D).astype(jnp.bfloat16)
    return (context, compact(reached, leaf_one, new_kv))

def reference(hidden, tree_qkv, prompt_kv, prompt_len, private_kv, priv_len, parents, leaf, w_out, norm_gain, w_router, routes, w_gate_up, w_down):
    per_request = tree_qkv.reshape(REQUESTS, TREE, 3 * D)

    def run_request(operands):
        return one_request(operands[0], operands[1], operands[2], operands[3], operands[4], operands[5], prompt_kv, prompt_len)
    context, accepted_kv = lax.map(run_request, (jnp.arange(REQUESTS, dtype=jnp.int32), per_request, private_kv, priv_len, parents, leaf))
    context = context.reshape(TOKENS, D)
    attended = jnp.dot(context, w_out, preferred_element_type=jnp.float32)
    middle = (hidden.astype(jnp.float32) + attended).astype(jnp.bfloat16)
    middle32 = middle.astype(jnp.float32)
    normed = (middle32 * lax.rsqrt(lax.optimization_barrier(jnp.mean(middle32 * middle32, axis=1, keepdims=True)) + EPS) * norm_gain).astype(jnp.bfloat16)
    logits = jnp.dot(normed, w_router, preferred_element_type=jnp.float32)
    picked = jnp.take_along_axis(logits, routes, axis=1)
    gate_first = jax.nn.sigmoid(picked[:, 0] - picked[:, 1])
    gate_second = jax.nn.sigmoid(picked[:, 1] - picked[:, 0])
    dev_rows = REQ_DEV * TREE
    devices = TOKENS // dev_rows
    onehot = (routes[:, :, None] == jnp.arange(EXPERTS, dtype=jnp.int32)[None, None, :]).astype(jnp.int32).reshape(devices, 2 * dev_rows, EXPERTS)
    slot_rank = lax.optimization_barrier(jnp.sum((jnp.cumsum(onehot, axis=1) - onehot) * onehot, axis=2)).reshape(2 * TOKENS)
    device_of = jnp.arange(2 * TOKENS, dtype=jnp.int32) // (2 * dev_rows)
    slot_place = device_of * CAP + slot_rank
    expert_of = routes.reshape(2 * TOKENS)
    doubled = jnp.repeat(normed, 2, axis=0)
    buffers = jnp.zeros((EXPERTS, devices * CAP, D), jnp.bfloat16).at[expert_of, slot_place].set(doubled)

    def run_expert(operands):
        tokens_in, gate_up, down_rows = operands
        gate_act = jnp.dot(tokens_in, gate_up[0], preferred_element_type=jnp.float32)
        upper = jnp.dot(tokens_in, gate_up[1], preferred_element_type=jnp.float32)
        hidden_units = (jax.nn.silu(gate_act) * upper).astype(jnp.bfloat16)
        pieces = hidden_units.reshape(-1, N_DP, FF // N_DP).transpose(1, 0, 2)
        down_blocks = down_rows.reshape(N_DP, FF // N_DP, D)

        def add_piece(total_sum, pair_rows):
            term = jnp.dot(pair_rows[0], pair_rows[1], preferred_element_type=jnp.float32).astype(jnp.bfloat16)
            term = lax.optimization_barrier(term)
            return (total_sum + term.astype(jnp.float32), None)
        total_sum, unused_out = lax.scan(add_piece, jnp.zeros((tokens_in.shape[0], D), jnp.float32), (pieces, down_blocks))
        return total_sum
    results = lax.map(run_expert, (buffers, w_gate_up, w_down))
    fetched = results[expert_of, slot_place].reshape(TOKENS, 2, D)
    layer_out = (middle32 + gate_first[:, None] * fetched[:, 0] + gate_second[:, None] * fetched[:, 1]).astype(jnp.bfloat16)
    return (layer_out, accepted_kv)
```

```python
import functools
import math

import jax
import jax.numpy as jnp
from jax import lax
from jax.sharding import PartitionSpec as P

H = 36
HD = 64
TREE = 64
REQ_DEV = 1


NEG = -1e30
EPS = 1e-05
HIGH = lax.Precision.HIGHEST


def closure(parents):
    count = parents.shape[-1]
    columns = jnp.arange(count, dtype=jnp.int32)
    reached = (parents[:, :, None] == columns[None, None, :]).astype(jnp.float32) + jnp.eye(
        count, dtype=jnp.float32
    )[None]
    for sweeps in range((count - 1).bit_length()):
        reached = jnp.minimum(jnp.einsum("rij,rjk->rik", reached, reached, precision=HIGH), 1.0)
    return reached


def compact(reach_one, leaf_one, kv_one):
    count = reach_one.shape[0]
    marked = jnp.sum(
        jnp.where(jnp.arange(count, dtype=jnp.int32)[:, None] == leaf_one, reach_one, 0.0), axis=0
    )
    earlier = (
        jnp.arange(count, dtype=jnp.int32)[None, :] < jnp.arange(count, dtype=jnp.int32)[:, None]
    ).astype(jnp.float32)
    ordinal = jnp.dot(earlier, marked, precision=HIGH)
    slot_ids = jnp.arange(count, dtype=jnp.int32).astype(jnp.float32)
    chosen = jnp.where(slot_ids[:, None] == ordinal[None, :], marked[None, :], 0.0)
    return jnp.dot(chosen.astype(jnp.bfloat16), kv_one, preferred_element_type=jnp.float32).astype(
        jnp.bfloat16
    )


def partial_attention(query_matrix_rows, cache_rows, allowed):
    features = cache_rows.shape[1] // 2
    slots = cache_rows.shape[0]
    key_matrix_rows = cache_rows[:, :features].reshape(slots, H, HD)
    value_matrix_rows = cache_rows[:, features:].reshape(slots, H, HD)
    attention_score_scale = 1.0 / math.sqrt(HD)
    attention_scores = (
        jnp.einsum(
            "was,zas->waz", query_matrix_rows, key_matrix_rows, preferred_element_type=jnp.float32
        )
        * attention_score_scale
    )
    widened = allowed[:, None, :]
    attention_scores = jnp.where(widened, attention_scores, NEG)
    maxima = jnp.max(attention_scores, axis=-1)
    attention_weights = jnp.where(widened, jnp.exp(attention_scores - maxima[..., None]), 0.0)
    totals = jnp.sum(attention_weights, axis=-1)
    weighted_sum = jnp.einsum(
        "ubj,jbx->ubx",
        attention_weights.astype(jnp.bfloat16),
        value_matrix_rows,
        preferred_element_type=jnp.float32,
    )
    return (maxima, totals, weighted_sum)


def join_parts(first_part, second_part):
    highest = jnp.maximum(first_part[0], second_part[0])
    scale_first = jnp.exp(first_part[0] - highest)
    scale_second = jnp.exp(second_part[0] - highest)
    totals = first_part[1] * scale_first + second_part[1] * scale_second
    weighted_sum = first_part[2] * scale_first[..., None] + second_part[2] * scale_second[..., None]
    return (highest, totals, weighted_sum)


def as_rows(part_state, row_count):
    return (
        part_state[0].reshape(row_count, H),
        part_state[1].reshape(row_count, H),
        part_state[2].reshape(row_count, H, HD),
    )


def dp_ring(mesh):
    count = mesh.shape["dp"]
    try:
        axis = list(mesh.axis_names).index("dp")
        places = [tuple(mesh.devices.take(i, axis=axis).reshape(-1)[0].coords) for i in range(count)]
        varying = [a for a in range(len(places[0])) if len({c[a] for c in places}) > 1]
        changes = {a: sum(places[i][a] != places[i + 1][a] for i in range(count - 1)) for a in varying}
        slow, fast = sorted(varying, key=lambda a: changes[a])
        rows = sorted({c[slow] for c in places})
        cols = sorted({c[fast] for c in places})
        where = {(c[slow], c[fast]): i for i, c in enumerate(places)}
        if len(varying) != 2 or len(rows) * len(cols) != count or len(rows) % 2 or len(cols) < 2:
            raise ValueError
        cycle = [where[(rows[0], cols[0])]]
        for r, row in enumerate(rows):
            ordered = cols[1:] if r % 2 == 0 else cols[1:][::-1]
            cycle += [where[(row, col)] for col in ordered]
        cycle += [where[(row, cols[0])] for row in rows[1:][::-1]]
        if sorted(cycle) != list(range(count)):
            raise ValueError
        return cycle
    except Exception:
        return list(range(count))


def ring_gather(piece, ring, step):
    count = len(ring)
    pairs = [(ring[p], ring[(p + step) % count]) for p in range(count)]
    arrived = [piece]
    for unused in range(count - 1):
        piece = lax.ppermute(piece, "dp", pairs)
        arrived.append(piece)
    return arrived


def ring_reduce(blocks, ring, step):
    count = len(ring)
    pairs = [(ring[p], ring[(p + step) % count]) for p in range(count)]
    moving = blocks[1]
    for index in range(2, count):
        received = lax.ppermute(moving, "dp", pairs).astype(jnp.float32)
        moving = (received + blocks[index].astype(jnp.float32)).astype(jnp.bfloat16)
    received = lax.ppermute(moving, "dp", pairs).astype(jnp.float32)
    return received + blocks[0].astype(jnp.float32)


def local(
    ring,
    hidden,
    tree_qkv,
    prompt_kv,
    prompt_len,
    private_kv,
    priv_len,
    parents,
    leaf,
    w_out,
    norm_gain,
    w_router,
    routes,
    w_gate_up,
    w_down,
):
    row_count = hidden.shape[0]
    features = hidden.shape[1]
    query_vectors = tree_qkv[:, :features].reshape(row_count, H, HD)
    new_kv = tree_qkv[:, features:]
    reached = closure(parents)
    grouped_q = query_vectors.reshape(REQ_DEV, TREE, H, HD)
    grouped_kv = new_kv.reshape(REQ_DEV, TREE, 2 * features)
    tree_part = jax.vmap(partial_attention)(grouped_q, grouped_kv, reached > 0.5)
    private_slots = jnp.arange(private_kv.shape[1], dtype=jnp.int32)
    private_ok = jnp.broadcast_to(
        (private_slots[None, :] < priv_len[:, None])[:, None, :],
        (REQ_DEV, TREE, private_kv.shape[1]),
    )
    private_part = jax.vmap(partial_attention)(grouped_q, private_kv, private_ok)
    local_state = join_parts(as_rows(tree_part, row_count), as_rows(private_part, row_count))
    prompt_limit = prompt_len[0]
    start_state = (
        jnp.full((row_count, H), NEG, jnp.float32),
        jnp.zeros((row_count, H), jnp.float32),
        jnp.zeros((row_count, H, HD), jnp.float32),
    )
    shard_rows = lax.all_gather(prompt_kv, "expert", axis=1, tiled=True)
    piece_len = shard_rows.shape[1]
    places = jnp.arange(piece_len, dtype=jnp.int32)
    allowed = jnp.broadcast_to((places < prompt_limit)[None, :], (row_count, piece_len))
    prompt_state = join_parts(start_state, partial_attention(query_vectors, shard_rows[0], allowed))
    final_state = join_parts(local_state, prompt_state)
    context = (
        (final_state[2] / final_state[1][..., None])
        .reshape(row_count, features)
        .astype(jnp.bfloat16)
    )
    attended = jnp.dot(context, w_out, preferred_element_type=jnp.float32)
    middle = (hidden.astype(jnp.float32) + attended).astype(jnp.bfloat16)
    middle32 = middle.astype(jnp.float32)
    normed = (
        middle32 * lax.rsqrt(jnp.mean(middle32 * middle32, axis=1, keepdims=True) + EPS) * norm_gain
    ).astype(jnp.bfloat16)
    logits = jnp.dot(normed, w_router, preferred_element_type=jnp.float32)
    experts = w_router.shape[1]
    choose = routes[:, :, None] == jnp.arange(experts, dtype=jnp.int32)[None, None, :]
    picked = jnp.sum(jnp.where(choose, logits[:, None, :], 0.0), axis=2)
    gate_first = jax.nn.sigmoid(picked[:, 0] - picked[:, 1])
    gate_second = jax.nn.sigmoid(picked[:, 1] - picked[:, 0])
    capacity = 3 * row_count // experts
    onehot = choose.reshape(2 * row_count, experts).astype(jnp.float32)
    assign_ids = jnp.arange(2 * row_count, dtype=jnp.int32)
    earlier = (assign_ids[None, :] < assign_ids[:, None]).astype(jnp.float32)
    before = jnp.dot(earlier, onehot, precision=HIGH)
    slot_rank = jnp.sum(before * onehot, axis=1).astype(jnp.int32)
    target = routes.reshape(2 * row_count) * capacity + slot_rank
    select = (jnp.arange(experts * capacity, dtype=jnp.int32)[:, None] == target[None, :]).astype(
        jnp.bfloat16
    )
    doubled = jnp.repeat(normed, 2, axis=0)
    outgoing = (
        jnp.dot(select, doubled, preferred_element_type=jnp.float32)
        .astype(jnp.bfloat16)
        .reshape(experts, capacity, features)
    )
    gate_cols = w_gate_up[0, 0]
    up_cols = w_gate_up[0, 1]
    down_rows = w_down[0]
    arrived = lax.all_to_all(outgoing, "expert", split_axis=0, concat_axis=0, tiled=True)
    arrived = arrived.reshape(experts * capacity, features)
    half = experts * capacity // 2
    forward = ring_gather(arrived[:half], ring, 1)
    backward = ring_gather(arrived[half:], ring, -1)
    forward_out = []
    backward_out = []
    for index in range(len(ring)):
        pooled = jnp.concatenate([forward[index], backward[index]], axis=0)
        gate_act = jnp.dot(pooled, gate_cols, preferred_element_type=jnp.float32)
        upper = jnp.dot(pooled, up_cols, preferred_element_type=jnp.float32)
        hidden_units = (jax.nn.silu(gate_act) * upper).astype(jnp.bfloat16)
        partial = jnp.dot(hidden_units, down_rows, preferred_element_type=jnp.float32).astype(jnp.bfloat16)
        forward_out.append(partial[:half])
        backward_out.append(partial[half:])
    summed_rows = jnp.concatenate(
        [ring_reduce(forward_out, ring, 1), ring_reduce(backward_out, ring, -1)], axis=0
    )
    returned = lax.all_to_all(
        summed_rows.reshape(experts, capacity, features).astype(jnp.bfloat16),
        "expert",
        split_axis=0,
        concat_axis=0,
        tiled=True,
    ).astype(jnp.float32)
    flat_back = returned.reshape(experts * capacity, features)
    fetched = jnp.take(flat_back, target, axis=0).reshape(row_count, 2, features)
    layer_out = (
        middle32 + gate_first[:, None] * fetched[:, 0] + gate_second[:, None] * fetched[:, 1]
    ).astype(jnp.bfloat16)
    accepted_kv = jax.vmap(compact)(reached, leaf, grouped_kv)
    return (layer_out, accepted_kv)


def solution(mesh):
    placed = (
        P(("dp", "expert"), None),
        P(("dp", "expert"), None),
        P("dp", "expert", None),
        P("dp"),
        P(("dp", "expert"), None, None),
        P(("dp", "expert")),
        P(("dp", "expert"), None),
        P(("dp", "expert")),
        P(),
        P(),
        P(),
        P(("dp", "expert"), None),
        P("expert", None, None, "dp"),
        P("expert", "dp", None),
    )
    ring = dp_ring(mesh)
    return jax.shard_map(
        functools.partial(local, ring),
        mesh=mesh,
        in_specs=placed,
        out_specs=(P(("dp", "expert"), None), P(("dp", "expert"), None, None)),
        check_vma=False,
    )
```

```python
import functools
import math

import jax
import jax.numpy as jnp
from jax import lax
from jax.experimental import pallas as pl
from jax.sharding import PartitionSpec as P

H = 36
HD = 64
TREE = 64
REQ_DEV = 1


NEG = -1e30
EPS = 1e-05
HIGH = lax.Precision.HIGHEST


def closure(parents):
    count = parents.shape[-1]
    columns = jnp.arange(count, dtype=jnp.int32)
    reached = (parents[:, :, None] == columns[None, None, :]).astype(jnp.float32) + jnp.eye(
        count, dtype=jnp.float32
    )[None]
    for sweeps in range((count - 1).bit_length()):
        reached = jnp.minimum(jnp.einsum("rij,rjk->rik", reached, reached, precision=HIGH), 1.0)
    return reached


def compact(reach_one, leaf_one, kv_one):
    count = reach_one.shape[0]
    marked = jnp.sum(
        jnp.where(jnp.arange(count, dtype=jnp.int32)[:, None] == leaf_one, reach_one, 0.0), axis=0
    )
    earlier = (
        jnp.arange(count, dtype=jnp.int32)[None, :] < jnp.arange(count, dtype=jnp.int32)[:, None]
    ).astype(jnp.float32)
    ordinal = jnp.dot(earlier, marked, precision=HIGH)
    slot_ids = jnp.arange(count, dtype=jnp.int32).astype(jnp.float32)
    chosen = jnp.where(slot_ids[:, None] == ordinal[None, :], marked[None, :], 0.0)
    return jnp.dot(chosen.astype(jnp.bfloat16), kv_one, preferred_element_type=jnp.float32).astype(
        jnp.bfloat16
    )


def partial_attention(query_matrix_rows, cache_rows, allowed):
    features = cache_rows.shape[1] // 2
    slots = cache_rows.shape[0]
    key_matrix_rows = cache_rows[:, :features].reshape(slots, H, HD)
    value_matrix_rows = cache_rows[:, features:].reshape(slots, H, HD)
    attention_score_scale = 1.0 / math.sqrt(HD)
    attention_scores = (
        jnp.einsum(
            "was,zas->waz", query_matrix_rows, key_matrix_rows, preferred_element_type=jnp.float32
        )
        * attention_score_scale
    )
    widened = allowed[:, None, :]
    attention_scores = jnp.where(widened, attention_scores, NEG)
    maxima = jnp.max(attention_scores, axis=-1)
    attention_weights = jnp.where(widened, jnp.exp(attention_scores - maxima[..., None]), 0.0)
    totals = jnp.sum(attention_weights, axis=-1)
    weighted_sum = jnp.einsum(
        "ubj,jbx->ubx",
        attention_weights.astype(jnp.bfloat16),
        value_matrix_rows,
        preferred_element_type=jnp.float32,
    )
    return (maxima, totals, weighted_sum)


def join_parts(first_part, second_part):
    highest = jnp.maximum(first_part[0], second_part[0])
    scale_first = jnp.exp(first_part[0] - highest)
    scale_second = jnp.exp(second_part[0] - highest)
    totals = first_part[1] * scale_first + second_part[1] * scale_second
    weighted_sum = first_part[2] * scale_first[..., None] + second_part[2] * scale_second[..., None]
    return (highest, totals, weighted_sum)


def as_rows(part_state, row_count):
    return (
        part_state[0].reshape(row_count, H),
        part_state[1].reshape(row_count, H),
        part_state[2].reshape(row_count, H, HD),
    )


def attend_kernel(*refs, count, scale):
    q_ref = refs[0]
    sources = refs[1:1 + 3 * count]
    acc_ref, top_ref, total_ref = refs[1 + 3 * count:]
    width = q_ref.shape[1] // 2
    for head in range(2):
        cols = slice(head * width, (head + 1) * width)
        query = q_ref[:, cols]
        scores = []
        for index in range(count):
            keys = sources[3 * index][:, cols]
            raw = lax.dot_general(
                query, keys, (((1,), (1,)), ((), ())), preferred_element_type=jnp.float32
            ) * scale
            scores.append(jnp.where(sources[3 * index + 2][...] > 0.5, raw, NEG))
        top = scores[0].max(axis=1, keepdims=True)
        for more in scores[1:]:
            top = jnp.maximum(top, more.max(axis=1, keepdims=True))
        total = jnp.zeros_like(top)
        acc = jnp.zeros((query.shape[0], width), jnp.float32)
        for index in range(count):
            weights = jnp.where(sources[3 * index + 2][...] > 0.5, jnp.exp(scores[index] - top), 0.0)
            total = total + weights.sum(axis=1, keepdims=True)
            acc = acc + jnp.dot(
                weights.astype(jnp.bfloat16),
                sources[3 * index + 1][:, cols],
                preferred_element_type=jnp.float32,
            )
        acc_ref[:, cols] = acc
        top_ref[:, cols] = jnp.broadcast_to(top, acc.shape)
        total_ref[:, cols] = jnp.broadcast_to(total, acc.shape)


def attend(query_rows, sources):
    rows, features = query_rows.shape
    pairs = features // (2 * HD)
    block = 2 * HD
    operands = [query_rows]
    specs = [pl.BlockSpec((rows, block), lambda h: (0, h))]
    for table, key_offset, value_offset, allowed in sources:
        slots = table.shape[0]
        operands += [table, table, allowed.astype(jnp.float32)]
        specs += [
            pl.BlockSpec((slots, block), lambda h, o=key_offset: (0, o + h)),
            pl.BlockSpec((slots, block), lambda h, o=value_offset: (0, o + h)),
            pl.BlockSpec((rows, slots), lambda h: (0, 0)),
        ]
    shape = jax.ShapeDtypeStruct((rows, features), jnp.float32)
    out_spec = pl.BlockSpec((rows, block), lambda h: (0, h))
    return pl.pallas_call(
        functools.partial(attend_kernel, count=len(sources), scale=1.0 / math.sqrt(HD)),
        grid=(pairs,),
        in_specs=specs,
        out_specs=(out_spec, out_spec, out_spec),
        out_shape=(shape, shape, shape),
    )(*operands)


def dp_ring(mesh):
    count = mesh.shape["dp"]
    try:
        axis = list(mesh.axis_names).index("dp")
        places = [tuple(mesh.devices.take(i, axis=axis).reshape(-1)[0].coords) for i in range(count)]
        varying = [a for a in range(len(places[0])) if len({c[a] for c in places}) > 1]
        changes = {a: sum(places[i][a] != places[i + 1][a] for i in range(count - 1)) for a in varying}
        slow, fast = sorted(varying, key=lambda a: changes[a])
        rows = sorted({c[slow] for c in places})
        cols = sorted({c[fast] for c in places})
        where = {(c[slow], c[fast]): i for i, c in enumerate(places)}
        if len(varying) != 2 or len(rows) * len(cols) != count or len(rows) % 2 or len(cols) < 2:
            raise ValueError
        cycle = [where[(rows[0], cols[0])]]
        for r, row in enumerate(rows):
            ordered = cols[1:] if r % 2 == 0 else cols[1:][::-1]
            cycle += [where[(row, col)] for col in ordered]
        cycle += [where[(row, cols[0])] for row in rows[1:][::-1]]
        if sorted(cycle) != list(range(count)):
            raise ValueError
        return cycle
    except Exception:
        return list(range(count))


def ring_gather(piece, ring, step):
    count = len(ring)
    pairs = [(ring[p], ring[(p + step) % count]) for p in range(count)]
    arrived = [piece]
    for unused in range(count - 1):
        piece = lax.ppermute(piece, "dp", pairs)
        arrived.append(piece)
    return arrived


def ring_reduce(blocks, ring, step):
    count = len(ring)
    pairs = [(ring[p], ring[(p + step) % count]) for p in range(count)]
    moving = blocks[1]
    for index in range(2, count):
        received = lax.ppermute(moving, "dp", pairs).astype(jnp.float32)
        moving = (received + blocks[index].astype(jnp.float32)).astype(jnp.bfloat16)
    received = lax.ppermute(moving, "dp", pairs).astype(jnp.float32)
    return received + blocks[0].astype(jnp.float32)


def local(
    ring,
    hidden,
    tree_qkv,
    prompt_kv,
    prompt_len,
    private_kv,
    priv_len,
    parents,
    leaf,
    w_out,
    norm_gain,
    w_router,
    routes,
    w_gate_up,
    w_down,
):
    row_count = hidden.shape[0]
    features = hidden.shape[1]
    new_kv = tree_qkv[:, features:]
    reached = closure(parents)
    grouped_kv = new_kv.reshape(REQ_DEV, TREE, 2 * features)
    blocks = features // (2 * HD)
    private_slots = jnp.arange(private_kv.shape[1], dtype=jnp.int32)
    private_ok = jnp.broadcast_to(private_slots[None, :] < priv_len[0], (row_count, private_kv.shape[1]))
    local_acc, local_top, local_total = attend(
        tree_qkv[:, :features],
        [
            (private_kv[0], 0, blocks, private_ok),
            (tree_qkv, blocks, 2 * blocks, reached[0] > 0.5),
        ],
    )
    shard_rows = lax.all_gather(prompt_kv, "expert", axis=1, tiled=True)
    piece_len = shard_rows.shape[1]
    places = jnp.arange(piece_len, dtype=jnp.int32)
    prompt_ok = jnp.broadcast_to((places < prompt_len[0])[None, :], (row_count, piece_len))
    prompt_acc, prompt_top, prompt_total = attend(
        tree_qkv[:, :features], [(shard_rows[0], 0, blocks, prompt_ok)]
    )
    highest = jnp.maximum(local_top, prompt_top)
    scale_local = jnp.exp(local_top - highest)
    scale_prompt = jnp.exp(prompt_top - highest)
    totals = local_total * scale_local + prompt_total * scale_prompt
    weighted = local_acc * scale_local + prompt_acc * scale_prompt
    context = (weighted / totals).astype(jnp.bfloat16)
    attended = jnp.dot(context, w_out, preferred_element_type=jnp.float32)
    middle = (hidden.astype(jnp.float32) + attended).astype(jnp.bfloat16)
    middle32 = middle.astype(jnp.float32)
    normed = (
        middle32 * lax.rsqrt(jnp.mean(middle32 * middle32, axis=1, keepdims=True) + EPS) * norm_gain
    ).astype(jnp.bfloat16)
    logits = jnp.dot(normed, w_router, preferred_element_type=jnp.float32)
    experts = w_router.shape[1]
    choose = routes[:, :, None] == jnp.arange(experts, dtype=jnp.int32)[None, None, :]
    picked = jnp.sum(jnp.where(choose, logits[:, None, :], 0.0), axis=2)
    gate_first = jax.nn.sigmoid(picked[:, 0] - picked[:, 1])
    gate_second = jax.nn.sigmoid(picked[:, 1] - picked[:, 0])
    capacity = 3 * row_count // experts
    onehot = choose.reshape(2 * row_count, experts).astype(jnp.float32)
    assign_ids = jnp.arange(2 * row_count, dtype=jnp.int32)
    earlier = (assign_ids[None, :] < assign_ids[:, None]).astype(jnp.float32)
    before = jnp.dot(earlier, onehot, precision=HIGH)
    slot_rank = jnp.sum(before * onehot, axis=1).astype(jnp.int32)
    target = routes.reshape(2 * row_count) * capacity + slot_rank
    select = (jnp.arange(experts * capacity, dtype=jnp.int32)[:, None] == target[None, :]).astype(
        jnp.bfloat16
    )
    doubled = jnp.repeat(normed, 2, axis=0)
    outgoing = (
        jnp.dot(select, doubled, preferred_element_type=jnp.float32)
        .astype(jnp.bfloat16)
        .reshape(experts, capacity, features)
    )
    gate_cols = w_gate_up[0, 0]
    up_cols = w_gate_up[0, 1]
    down_rows = w_down[0]
    arrived = lax.all_to_all(outgoing, "expert", split_axis=0, concat_axis=0, tiled=True)
    arrived = arrived.reshape(experts * capacity, features)
    half = experts * capacity // 2
    forward = ring_gather(arrived[:half], ring, 1)
    backward = ring_gather(arrived[half:], ring, -1)
    forward_out = []
    backward_out = []
    for index in range(len(ring)):
        pooled = jnp.concatenate([forward[index], backward[index]], axis=0)
        gate_act = jnp.dot(pooled, gate_cols, preferred_element_type=jnp.float32)
        upper = jnp.dot(pooled, up_cols, preferred_element_type=jnp.float32)
        hidden_units = (jax.nn.silu(gate_act) * upper).astype(jnp.bfloat16)
        partial = jnp.dot(hidden_units, down_rows, preferred_element_type=jnp.float32).astype(jnp.bfloat16)
        forward_out.append(partial[:half])
        backward_out.append(partial[half:])
    summed_rows = jnp.concatenate(
        [ring_reduce(forward_out, ring, 1), ring_reduce(backward_out, ring, -1)], axis=0
    )
    returned = lax.all_to_all(
        summed_rows.reshape(experts, capacity, features).astype(jnp.bfloat16),
        "expert",
        split_axis=0,
        concat_axis=0,
        tiled=True,
    ).astype(jnp.float32)
    flat_back = returned.reshape(experts * capacity, features)
    fetched = jnp.take(flat_back, target, axis=0).reshape(row_count, 2, features)
    layer_out = (
        middle32 + gate_first[:, None] * fetched[:, 0] + gate_second[:, None] * fetched[:, 1]
    ).astype(jnp.bfloat16)
    accepted_kv = jax.vmap(compact)(reached, leaf, grouped_kv)
    return (layer_out, accepted_kv)


def solution(mesh):
    placed = (
        P(("dp", "expert"), None),
        P(("dp", "expert"), None),
        P("dp", "expert", None),
        P("dp"),
        P(("dp", "expert"), None, None),
        P(("dp", "expert")),
        P(("dp", "expert"), None),
        P(("dp", "expert")),
        P(),
        P(),
        P(),
        P(("dp", "expert"), None),
        P("expert", None, None, "dp"),
        P("expert", "dp", None),
    )
    ring = dp_ring(mesh)
    return jax.shard_map(
        functools.partial(local, ring),
        mesh=mesh,
        in_specs=placed,
        out_specs=(P(("dp", "expert"), None), P(("dp", "expert"), None, None)),
        check_vma=False,
    )
```

```python
import functools
import math

import jax
import jax.numpy as jnp
from jax import lax
from jax.experimental import pallas as pl
from jax.sharding import PartitionSpec as P

H = 36
HD = 64
TREE = 64
REQ_DEV = 1


NEG = -1e30
EPS = 1e-05
HIGH = lax.Precision.HIGHEST


def closure(parents):
    count = parents.shape[-1]
    columns = jnp.arange(count, dtype=jnp.int32)
    reached = (parents[:, :, None] == columns[None, None, :]).astype(jnp.float32) + jnp.eye(
        count, dtype=jnp.float32
    )[None]
    for sweeps in range((count - 1).bit_length()):
        reached = jnp.minimum(jnp.einsum("rij,rjk->rik", reached, reached, precision=HIGH), 1.0)
    return reached


def compact(reach_one, leaf_one, kv_one):
    count = reach_one.shape[0]
    marked = jnp.sum(
        jnp.where(jnp.arange(count, dtype=jnp.int32)[:, None] == leaf_one, reach_one, 0.0), axis=0
    )
    earlier = (
        jnp.arange(count, dtype=jnp.int32)[None, :] < jnp.arange(count, dtype=jnp.int32)[:, None]
    ).astype(jnp.float32)
    ordinal = jnp.dot(earlier, marked, precision=HIGH)
    slot_ids = jnp.arange(count, dtype=jnp.int32).astype(jnp.float32)
    chosen = jnp.where(slot_ids[:, None] == ordinal[None, :], marked[None, :], 0.0)
    return jnp.dot(chosen.astype(jnp.bfloat16), kv_one, preferred_element_type=jnp.float32).astype(
        jnp.bfloat16
    )


def partial_attention(query_matrix_rows, cache_rows, allowed):
    features = cache_rows.shape[1] // 2
    slots = cache_rows.shape[0]
    key_matrix_rows = cache_rows[:, :features].reshape(slots, H, HD)
    value_matrix_rows = cache_rows[:, features:].reshape(slots, H, HD)
    attention_score_scale = 1.0 / math.sqrt(HD)
    attention_scores = (
        jnp.einsum(
            "was,zas->waz", query_matrix_rows, key_matrix_rows, preferred_element_type=jnp.float32
        )
        * attention_score_scale
    )
    widened = allowed[:, None, :]
    attention_scores = jnp.where(widened, attention_scores, NEG)
    maxima = jnp.max(attention_scores, axis=-1)
    attention_weights = jnp.where(widened, jnp.exp(attention_scores - maxima[..., None]), 0.0)
    totals = jnp.sum(attention_weights, axis=-1)
    weighted_sum = jnp.einsum(
        "ubj,jbx->ubx",
        attention_weights.astype(jnp.bfloat16),
        value_matrix_rows,
        preferred_element_type=jnp.float32,
    )
    return (maxima, totals, weighted_sum)


def join_parts(first_part, second_part):
    highest = jnp.maximum(first_part[0], second_part[0])
    scale_first = jnp.exp(first_part[0] - highest)
    scale_second = jnp.exp(second_part[0] - highest)
    totals = first_part[1] * scale_first + second_part[1] * scale_second
    weighted_sum = first_part[2] * scale_first[..., None] + second_part[2] * scale_second[..., None]
    return (highest, totals, weighted_sum)


def as_rows(part_state, row_count):
    return (
        part_state[0].reshape(row_count, H),
        part_state[1].reshape(row_count, H),
        part_state[2].reshape(row_count, H, HD),
    )


def attend_kernel(*refs, count, scale):
    q_ref = refs[0]
    sources = refs[1:1 + 3 * count]
    acc_ref, top_ref, total_ref = refs[1 + 3 * count:]
    width = q_ref.shape[1] // 2
    for head in range(2):
        cols = slice(head * width, (head + 1) * width)
        query = q_ref[:, cols]
        scores = []
        for index in range(count):
            keys = sources[3 * index][:, cols]
            raw = lax.dot_general(
                query, keys, (((1,), (1,)), ((), ())), preferred_element_type=jnp.float32
            ) * scale
            scores.append(jnp.where(sources[3 * index + 2][...] > 0.5, raw, NEG))
        top = scores[0].max(axis=1, keepdims=True)
        for more in scores[1:]:
            top = jnp.maximum(top, more.max(axis=1, keepdims=True))
        total = jnp.zeros_like(top)
        acc = jnp.zeros((query.shape[0], width), jnp.float32)
        for index in range(count):
            weights = jnp.where(sources[3 * index + 2][...] > 0.5, jnp.exp(scores[index] - top), 0.0)
            total = total + weights.sum(axis=1, keepdims=True)
            acc = acc + jnp.dot(
                weights.astype(jnp.bfloat16),
                sources[3 * index + 1][:, cols],
                preferred_element_type=jnp.float32,
            )
        acc_ref[:, cols] = acc
        top_ref[:, cols] = jnp.broadcast_to(top, acc.shape)
        total_ref[:, cols] = jnp.broadcast_to(total, acc.shape)


def attend(query_rows, sources):
    rows, features = query_rows.shape
    pairs = features // (2 * HD)
    block = 2 * HD
    operands = [query_rows]
    specs = [pl.BlockSpec((rows, block), lambda h: (0, h))]
    for table, key_offset, value_offset, allowed in sources:
        slots = table.shape[0]
        operands += [table, table, allowed.astype(jnp.float32)]
        specs += [
            pl.BlockSpec((slots, block), lambda h, o=key_offset: (0, o + h)),
            pl.BlockSpec((slots, block), lambda h, o=value_offset: (0, o + h)),
            pl.BlockSpec((rows, slots), lambda h: (0, 0)),
        ]
    shape = jax.ShapeDtypeStruct((rows, features), jnp.float32)
    out_spec = pl.BlockSpec((rows, block), lambda h: (0, h))
    return pl.pallas_call(
        functools.partial(attend_kernel, count=len(sources), scale=1.0 / math.sqrt(HD)),
        grid=(pairs,),
        in_specs=specs,
        out_specs=(out_spec, out_spec, out_spec),
        out_shape=(shape, shape, shape),
    )(*operands)


def dp_ring(mesh):
    count = mesh.shape["dp"]
    try:
        axis = list(mesh.axis_names).index("dp")
        places = [tuple(mesh.devices.take(i, axis=axis).reshape(-1)[0].coords) for i in range(count)]
        varying = [a for a in range(len(places[0])) if len({c[a] for c in places}) > 1]
        changes = {a: sum(places[i][a] != places[i + 1][a] for i in range(count - 1)) for a in varying}
        slow, fast = sorted(varying, key=lambda a: changes[a])
        rows = sorted({c[slow] for c in places})
        cols = sorted({c[fast] for c in places})
        where = {(c[slow], c[fast]): i for i, c in enumerate(places)}
        if len(varying) != 2 or len(rows) * len(cols) != count or len(rows) % 2 or len(cols) < 2:
            raise ValueError
        cycle = [where[(rows[0], cols[0])]]
        for r, row in enumerate(rows):
            ordered = cols[1:] if r % 2 == 0 else cols[1:][::-1]
            cycle += [where[(row, col)] for col in ordered]
        cycle += [where[(row, cols[0])] for row in rows[1:][::-1]]
        if sorted(cycle) != list(range(count)):
            raise ValueError
        return cycle
    except Exception:
        return list(range(count))


def ring_gather(piece, ring, step):
    count = len(ring)
    pairs = [(ring[p], ring[(p + step) % count]) for p in range(count)]
    arrived = [piece]
    for unused in range(count - 1):
        piece = lax.ppermute(piece, "dp", pairs)
        arrived.append(piece)
    return arrived


def ring_reduce(blocks, ring, step):
    count = len(ring)
    pairs = [(ring[p], ring[(p + step) % count]) for p in range(count)]
    moving = blocks[1]
    for index in range(2, count):
        received = lax.ppermute(moving, "dp", pairs).astype(jnp.float32)
        moving = (received + blocks[index].astype(jnp.float32)).astype(jnp.bfloat16)
    received = lax.ppermute(moving, "dp", pairs).astype(jnp.float32)
    return received + blocks[0].astype(jnp.float32)


def local(
    ring,
    hidden,
    tree_qkv,
    prompt_kv,
    prompt_len,
    private_kv,
    priv_len,
    parents,
    leaf,
    w_out,
    norm_gain,
    w_router,
    routes,
    w_gate_up,
    w_down,
):
    row_count = hidden.shape[0]
    features = hidden.shape[1]
    new_kv = tree_qkv[:, features:]
    reached = closure(parents)
    grouped_kv = new_kv.reshape(REQ_DEV, TREE, 2 * features)
    blocks = features // (2 * HD)
    private_slots = jnp.arange(private_kv.shape[1], dtype=jnp.int32)
    private_ok = jnp.broadcast_to(private_slots[None, :] < priv_len[0], (row_count, private_kv.shape[1]))
    local_acc, local_top, local_total = attend(
        tree_qkv[:, :features],
        [
            (private_kv[0], 0, blocks, private_ok),
            (tree_qkv, blocks, 2 * blocks, reached[0] > 0.5),
        ],
    )
    shard_rows = lax.all_gather(prompt_kv, "expert", axis=1, tiled=True)
    piece_len = shard_rows.shape[1]
    places = jnp.arange(piece_len, dtype=jnp.int32)
    prompt_ok = jnp.broadcast_to((places < prompt_len[0])[None, :], (row_count, piece_len))
    prompt_acc, prompt_top, prompt_total = attend(
        tree_qkv[:, :features], [(shard_rows[0], 0, blocks, prompt_ok)]
    )
    highest = jnp.maximum(local_top, prompt_top)
    scale_local = jnp.exp(local_top - highest)
    scale_prompt = jnp.exp(prompt_top - highest)
    totals = local_total * scale_local + prompt_total * scale_prompt
    weighted = local_acc * scale_local + prompt_acc * scale_prompt
    context = (weighted / totals).astype(jnp.bfloat16)
    attended = jnp.dot(context, w_out, preferred_element_type=jnp.float32)
    middle = (hidden.astype(jnp.float32) + attended).astype(jnp.bfloat16)
    middle32 = middle.astype(jnp.float32)
    normed = (
        middle32 * lax.rsqrt(jnp.mean(middle32 * middle32, axis=1, keepdims=True) + EPS) * norm_gain
    ).astype(jnp.bfloat16)
    logits = jnp.dot(normed, w_router, preferred_element_type=jnp.float32)
    experts = w_router.shape[1]
    choose = routes[:, :, None] == jnp.arange(experts, dtype=jnp.int32)[None, None, :]
    picked = jnp.sum(jnp.where(choose, logits[:, None, :], 0.0), axis=2)
    gate_first = jax.nn.sigmoid(picked[:, 0] - picked[:, 1])
    gate_second = jax.nn.sigmoid(picked[:, 1] - picked[:, 0])
    capacity = 3 * row_count // experts
    onehot = choose.reshape(2 * row_count, experts).astype(jnp.float32)
    assign_ids = jnp.arange(2 * row_count, dtype=jnp.int32)
    earlier = (assign_ids[None, :] < assign_ids[:, None]).astype(jnp.float32)
    before = jnp.dot(earlier, onehot, precision=HIGH)
    slot_rank = jnp.sum(before * onehot, axis=1).astype(jnp.int32)
    target = routes.reshape(2 * row_count) * capacity + slot_rank
    select = (jnp.arange(experts * capacity, dtype=jnp.int32)[:, None] == target[None, :]).astype(
        jnp.bfloat16
    )
    doubled = jnp.repeat(normed, 2, axis=0)
    outgoing = (
        jnp.dot(select, doubled, preferred_element_type=jnp.float32)
        .astype(jnp.bfloat16)
        .reshape(experts, capacity, features)
    )
    gate_cols = w_gate_up[0, 0]
    up_cols = w_gate_up[0, 1]
    down_rows = w_down[0]
    arrived = lax.all_to_all(outgoing, "expert", split_axis=0, concat_axis=0, tiled=True)
    arrived = arrived.reshape(experts * capacity, features)
    half = experts * capacity // 2
    forward = ring_gather(arrived[:half], ring, 1)
    backward = ring_gather(arrived[half:], ring, -1)
    forward_out = []
    backward_out = []
    together = 2 if len(ring) % 2 == 0 else 1
    for first in range(0, len(ring), together):
        chosen = range(first, first + together)
        pooled = jnp.concatenate(
            [forward[index] for index in chosen] + [backward[index] for index in chosen], axis=0
        )
        gate_act = jnp.dot(pooled, gate_cols, preferred_element_type=jnp.float32)
        upper = jnp.dot(pooled, up_cols, preferred_element_type=jnp.float32)
        hidden_units = (jax.nn.silu(gate_act) * upper).astype(jnp.bfloat16)
        partial = jnp.dot(hidden_units, down_rows, preferred_element_type=jnp.float32).astype(jnp.bfloat16)
        for offset in range(together):
            forward_out.append(partial[offset * half:(offset + 1) * half])
            backward_out.append(partial[(together + offset) * half:(together + offset + 1) * half])
    summed_rows = jnp.concatenate(
        [ring_reduce(forward_out, ring, 1), ring_reduce(backward_out, ring, -1)], axis=0
    )
    returned = lax.all_to_all(
        summed_rows.reshape(experts, capacity, features).astype(jnp.bfloat16),
        "expert",
        split_axis=0,
        concat_axis=0,
        tiled=True,
    ).astype(jnp.float32)
    flat_back = returned.reshape(experts * capacity, features)
    fetched = jnp.take(flat_back, target, axis=0).reshape(row_count, 2, features)
    layer_out = (
        middle32 + gate_first[:, None] * fetched[:, 0] + gate_second[:, None] * fetched[:, 1]
    ).astype(jnp.bfloat16)
    accepted_kv = jax.vmap(compact)(reached, leaf, grouped_kv)
    return (layer_out, accepted_kv)


def solution(mesh):
    placed = (
        P(("dp", "expert"), None),
        P(("dp", "expert"), None),
        P("dp", "expert", None),
        P("dp"),
        P(("dp", "expert"), None, None),
        P(("dp", "expert")),
        P(("dp", "expert"), None),
        P(("dp", "expert")),
        P(),
        P(),
        P(),
        P(("dp", "expert"), None),
        P("expert", None, None, "dp"),
        P("expert", "dp", None),
    )
    ring = dp_ring(mesh)
    return jax.shard_map(
        functools.partial(local, ring),
        mesh=mesh,
        in_specs=placed,
        out_specs=(P(("dp", "expert"), None), P(("dp", "expert"), None, None)),
        check_vma=False,
    )
```

```python
import functools
import math

import jax
import jax.numpy as jnp
from jax import lax
from jax.experimental import pallas as pl
from jax.sharding import PartitionSpec as P

H = 36
HD = 64
TREE = 64
REQ_DEV = 1


NEG = -1e30
EPS = 1e-05
HIGH = lax.Precision.HIGHEST


def closure(parents):
    count = parents.shape[-1]
    columns = jnp.arange(count, dtype=jnp.int32)
    reached = (parents[:, :, None] == columns[None, None, :]).astype(jnp.float32) + jnp.eye(
        count, dtype=jnp.float32
    )[None]
    for sweeps in range((count - 1).bit_length()):
        reached = jnp.minimum(jnp.einsum("rij,rjk->rik", reached, reached, precision=HIGH), 1.0)
    return reached


def compact(reach_one, leaf_one, kv_one):
    count = reach_one.shape[0]
    marked = jnp.sum(
        jnp.where(jnp.arange(count, dtype=jnp.int32)[:, None] == leaf_one, reach_one, 0.0), axis=0
    )
    earlier = (
        jnp.arange(count, dtype=jnp.int32)[None, :] < jnp.arange(count, dtype=jnp.int32)[:, None]
    ).astype(jnp.float32)
    ordinal = jnp.dot(earlier, marked, precision=HIGH)
    slot_ids = jnp.arange(count, dtype=jnp.int32).astype(jnp.float32)
    chosen = jnp.where(slot_ids[:, None] == ordinal[None, :], marked[None, :], 0.0)
    return jnp.dot(chosen.astype(jnp.bfloat16), kv_one, preferred_element_type=jnp.float32).astype(
        jnp.bfloat16
    )


def partial_attention(query_matrix_rows, cache_rows, allowed):
    features = cache_rows.shape[1] // 2
    slots = cache_rows.shape[0]
    key_matrix_rows = cache_rows[:, :features].reshape(slots, H, HD)
    value_matrix_rows = cache_rows[:, features:].reshape(slots, H, HD)
    attention_score_scale = 1.0 / math.sqrt(HD)
    attention_scores = (
        jnp.einsum(
            "was,zas->waz", query_matrix_rows, key_matrix_rows, preferred_element_type=jnp.float32
        )
        * attention_score_scale
    )
    widened = allowed[:, None, :]
    attention_scores = jnp.where(widened, attention_scores, NEG)
    maxima = jnp.max(attention_scores, axis=-1)
    attention_weights = jnp.where(widened, jnp.exp(attention_scores - maxima[..., None]), 0.0)
    totals = jnp.sum(attention_weights, axis=-1)
    weighted_sum = jnp.einsum(
        "ubj,jbx->ubx",
        attention_weights.astype(jnp.bfloat16),
        value_matrix_rows,
        preferred_element_type=jnp.float32,
    )
    return (maxima, totals, weighted_sum)


def join_parts(first_part, second_part):
    highest = jnp.maximum(first_part[0], second_part[0])
    scale_first = jnp.exp(first_part[0] - highest)
    scale_second = jnp.exp(second_part[0] - highest)
    totals = first_part[1] * scale_first + second_part[1] * scale_second
    weighted_sum = first_part[2] * scale_first[..., None] + second_part[2] * scale_second[..., None]
    return (highest, totals, weighted_sum)


def as_rows(part_state, row_count):
    return (
        part_state[0].reshape(row_count, H),
        part_state[1].reshape(row_count, H),
        part_state[2].reshape(row_count, H, HD),
    )


def attend_kernel(*refs, count, scale):
    q_ref = refs[0]
    sources = refs[1:1 + 3 * count]
    acc_ref, top_ref, total_ref = refs[1 + 3 * count:]
    width = HD
    for head in range(q_ref.shape[1] // HD):
        cols = slice(head * width, (head + 1) * width)
        query = q_ref[:, cols]
        scores = []
        for index in range(count):
            keys = sources[3 * index][:, cols]
            raw = lax.dot_general(
                query, keys, (((1,), (1,)), ((), ())), preferred_element_type=jnp.float32
            ) * scale
            scores.append(jnp.where(sources[3 * index + 2][...] > 0.5, raw, NEG))
        top = scores[0].max(axis=1, keepdims=True)
        for more in scores[1:]:
            top = jnp.maximum(top, more.max(axis=1, keepdims=True))
        total = jnp.zeros_like(top)
        acc = jnp.zeros((query.shape[0], width), jnp.float32)
        for index in range(count):
            weights = jnp.where(sources[3 * index + 2][...] > 0.5, jnp.exp(scores[index] - top), 0.0)
            total = total + weights.sum(axis=1, keepdims=True)
            acc = acc + jnp.dot(
                weights.astype(jnp.bfloat16),
                sources[3 * index + 1][:, cols],
                preferred_element_type=jnp.float32,
            )
        acc_ref[:, cols] = acc
        top_ref[:, cols] = jnp.broadcast_to(top, acc.shape)
        total_ref[:, cols] = jnp.broadcast_to(total, acc.shape)


def attend(query_rows, sources):
    rows, features = query_rows.shape
    group = 4 if (features // HD) % 4 == 0 else 2
    pairs = features // (group * HD)
    block = group * HD
    operands = [query_rows]
    specs = [pl.BlockSpec((rows, block), lambda h: (0, h))]
    for table, key_offset, value_offset, allowed in sources:
        slots = table.shape[0]
        operands += [table, table, allowed.astype(jnp.float32)]
        specs += [
            pl.BlockSpec((slots, block), lambda h, o=key_offset: (0, o + h)),
            pl.BlockSpec((slots, block), lambda h, o=value_offset: (0, o + h)),
            pl.BlockSpec((rows, slots), lambda h: (0, 0)),
        ]
    shape = jax.ShapeDtypeStruct((rows, features), jnp.float32)
    out_spec = pl.BlockSpec((rows, block), lambda h: (0, h))
    return pl.pallas_call(
        functools.partial(attend_kernel, count=len(sources), scale=1.0 / math.sqrt(HD)),
        grid=(pairs,),
        in_specs=specs,
        out_specs=(out_spec, out_spec, out_spec),
        out_shape=(shape, shape, shape),
    )(*operands)


def dp_ring(mesh):
    count = mesh.shape["dp"]
    try:
        axis = list(mesh.axis_names).index("dp")
        places = [tuple(mesh.devices.take(i, axis=axis).reshape(-1)[0].coords) for i in range(count)]
        varying = [a for a in range(len(places[0])) if len({c[a] for c in places}) > 1]
        changes = {a: sum(places[i][a] != places[i + 1][a] for i in range(count - 1)) for a in varying}
        slow, fast = sorted(varying, key=lambda a: changes[a])
        rows = sorted({c[slow] for c in places})
        cols = sorted({c[fast] for c in places})
        where = {(c[slow], c[fast]): i for i, c in enumerate(places)}
        if len(varying) != 2 or len(rows) * len(cols) != count or len(rows) % 2 or len(cols) < 2:
            raise ValueError
        cycle = [where[(rows[0], cols[0])]]
        for r, row in enumerate(rows):
            ordered = cols[1:] if r % 2 == 0 else cols[1:][::-1]
            cycle += [where[(row, col)] for col in ordered]
        cycle += [where[(row, cols[0])] for row in rows[1:][::-1]]
        if sorted(cycle) != list(range(count)):
            raise ValueError
        return cycle
    except Exception:
        return list(range(count))


def ring_gather(piece, ring, step):
    count = len(ring)
    pairs = [(ring[p], ring[(p + step) % count]) for p in range(count)]
    arrived = [piece]
    for unused in range(count - 1):
        piece = lax.ppermute(piece, "dp", pairs)
        arrived.append(piece)
    return arrived


def ring_reduce(blocks, ring, step):
    count = len(ring)
    pairs = [(ring[p], ring[(p + step) % count]) for p in range(count)]
    moving = blocks[1]
    for index in range(2, count):
        received = lax.ppermute(moving, "dp", pairs).astype(jnp.float32)
        moving = (received + blocks[index].astype(jnp.float32)).astype(jnp.bfloat16)
    received = lax.ppermute(moving, "dp", pairs).astype(jnp.float32)
    return received + blocks[0].astype(jnp.float32)


def local(
    ring,
    hidden,
    tree_qkv,
    prompt_kv,
    prompt_len,
    private_kv,
    priv_len,
    parents,
    leaf,
    w_out,
    norm_gain,
    w_router,
    routes,
    w_gate_up,
    w_down,
):
    row_count = hidden.shape[0]
    features = hidden.shape[1]
    new_kv = tree_qkv[:, features:]
    reached = closure(parents)
    grouped_kv = new_kv.reshape(REQ_DEV, TREE, 2 * features)
    blocks = features // ((4 if (features // HD) % 4 == 0 else 2) * HD)
    private_slots = jnp.arange(private_kv.shape[1], dtype=jnp.int32)
    private_ok = jnp.broadcast_to(private_slots[None, :] < priv_len[0], (row_count, private_kv.shape[1]))
    local_acc, local_top, local_total = attend(
        tree_qkv[:, :features],
        [
            (private_kv[0], 0, blocks, private_ok),
            (tree_qkv, blocks, 2 * blocks, reached[0] > 0.5),
        ],
    )
    shard_rows = lax.all_gather(prompt_kv, "expert", axis=1, tiled=True)
    piece_len = shard_rows.shape[1]
    places = jnp.arange(piece_len, dtype=jnp.int32)
    prompt_ok = jnp.broadcast_to((places < prompt_len[0])[None, :], (row_count, piece_len))
    prompt_acc, prompt_top, prompt_total = attend(
        tree_qkv[:, :features], [(shard_rows[0], 0, blocks, prompt_ok)]
    )
    highest = jnp.maximum(local_top, prompt_top)
    scale_local = jnp.exp(local_top - highest)
    scale_prompt = jnp.exp(prompt_top - highest)
    totals = local_total * scale_local + prompt_total * scale_prompt
    weighted = local_acc * scale_local + prompt_acc * scale_prompt
    context = (weighted / totals).astype(jnp.bfloat16)
    attended = jnp.dot(context, w_out, preferred_element_type=jnp.float32)
    middle = (hidden.astype(jnp.float32) + attended).astype(jnp.bfloat16)
    middle32 = middle.astype(jnp.float32)
    normed = (
        middle32 * lax.rsqrt(jnp.mean(middle32 * middle32, axis=1, keepdims=True) + EPS) * norm_gain
    ).astype(jnp.bfloat16)
    logits = jnp.dot(normed, w_router, preferred_element_type=jnp.float32)
    experts = w_router.shape[1]
    choose = routes[:, :, None] == jnp.arange(experts, dtype=jnp.int32)[None, None, :]
    picked = jnp.sum(jnp.where(choose, logits[:, None, :], 0.0), axis=2)
    gate_first = jax.nn.sigmoid(picked[:, 0] - picked[:, 1])
    gate_second = jax.nn.sigmoid(picked[:, 1] - picked[:, 0])
    capacity = 3 * row_count // experts
    onehot = choose.reshape(2 * row_count, experts).astype(jnp.float32)
    assign_ids = jnp.arange(2 * row_count, dtype=jnp.int32)
    earlier = (assign_ids[None, :] < assign_ids[:, None]).astype(jnp.float32)
    before = jnp.dot(earlier, onehot, precision=HIGH)
    slot_rank = jnp.sum(before * onehot, axis=1).astype(jnp.int32)
    target = routes.reshape(2 * row_count) * capacity + slot_rank
    select = (jnp.arange(experts * capacity, dtype=jnp.int32)[:, None] == target[None, :]).astype(
        jnp.bfloat16
    )
    doubled = jnp.repeat(normed, 2, axis=0)
    outgoing = (
        jnp.dot(select, doubled, preferred_element_type=jnp.float32)
        .astype(jnp.bfloat16)
        .reshape(experts, capacity, features)
    )
    gate_cols = w_gate_up[0, 0]
    up_cols = w_gate_up[0, 1]
    down_rows = w_down[0]
    arrived = lax.all_to_all(outgoing, "expert", split_axis=0, concat_axis=0, tiled=True)
    arrived = arrived.reshape(experts * capacity, features)
    half = experts * capacity // 2
    forward = ring_gather(arrived[:half], ring, 1)
    backward = ring_gather(arrived[half:], ring, -1)
    forward_out = []
    backward_out = []
    for index in range(len(ring)):
        pooled = jnp.concatenate([forward[index], backward[index]], axis=0)
        gate_act = jnp.dot(pooled, gate_cols, preferred_element_type=jnp.float32)
        upper = jnp.dot(pooled, up_cols, preferred_element_type=jnp.float32)
        hidden_units = (jax.nn.silu(gate_act) * upper).astype(jnp.bfloat16)
        partial = jnp.dot(hidden_units, down_rows, preferred_element_type=jnp.float32).astype(jnp.bfloat16)
        forward_out.append(partial[:half])
        backward_out.append(partial[half:])
    summed_rows = jnp.concatenate(
        [ring_reduce(forward_out, ring, 1), ring_reduce(backward_out, ring, -1)], axis=0
    )
    returned = lax.all_to_all(
        summed_rows.reshape(experts, capacity, features).astype(jnp.bfloat16),
        "expert",
        split_axis=0,
        concat_axis=0,
        tiled=True,
    ).astype(jnp.float32)
    flat_back = returned.reshape(experts * capacity, features)
    fetched = jnp.take(flat_back, target, axis=0).reshape(row_count, 2, features)
    layer_out = (
        middle32 + gate_first[:, None] * fetched[:, 0] + gate_second[:, None] * fetched[:, 1]
    ).astype(jnp.bfloat16)
    accepted_kv = jax.vmap(compact)(reached, leaf, grouped_kv)
    return (layer_out, accepted_kv)


def solution(mesh):
    placed = (
        P(("dp", "expert"), None),
        P(("dp", "expert"), None),
        P("dp", "expert", None),
        P("dp"),
        P(("dp", "expert"), None, None),
        P(("dp", "expert")),
        P(("dp", "expert"), None),
        P(("dp", "expert")),
        P(),
        P(),
        P(),
        P(("dp", "expert"), None),
        P("expert", None, None, "dp"),
        P("expert", "dp", None),
    )
    ring = dp_ring(mesh)
    return jax.shard_map(
        functools.partial(local, ring),
        mesh=mesh,
        in_specs=placed,
        out_specs=(P(("dp", "expert"), None), P(("dp", "expert"), None, None)),
        check_vma=False,
    )
```

```python
import functools
import math

import jax
import jax.numpy as jnp
from jax import lax
from jax.experimental import pallas as pl
from jax.experimental.pallas import tpu as pltpu
from jax.sharding import PartitionSpec as P

H = 36
HD = 64
TREE = 64
REQ_DEV = 1


NEG = -1e30
EPS = 1e-05
HIGH = lax.Precision.HIGHEST


def closure(parents):
    count = parents.shape[-1]
    columns = jnp.arange(count, dtype=jnp.int32)
    reached = (parents[:, :, None] == columns[None, None, :]).astype(jnp.float32) + jnp.eye(
        count, dtype=jnp.float32
    )[None]
    for sweeps in range((count - 1).bit_length()):
        reached = jnp.minimum(jnp.einsum("rij,rjk->rik", reached, reached, precision=HIGH), 1.0)
    return reached


def compact(reach_one, leaf_one, kv_one):
    count = reach_one.shape[0]
    marked = jnp.sum(
        jnp.where(jnp.arange(count, dtype=jnp.int32)[:, None] == leaf_one, reach_one, 0.0), axis=0
    )
    earlier = (
        jnp.arange(count, dtype=jnp.int32)[None, :] < jnp.arange(count, dtype=jnp.int32)[:, None]
    ).astype(jnp.float32)
    ordinal = jnp.dot(earlier, marked, precision=HIGH)
    slot_ids = jnp.arange(count, dtype=jnp.int32).astype(jnp.float32)
    chosen = jnp.where(slot_ids[:, None] == ordinal[None, :], marked[None, :], 0.0)
    return jnp.dot(chosen.astype(jnp.bfloat16), kv_one, preferred_element_type=jnp.float32).astype(
        jnp.bfloat16
    )


def partial_attention(query_matrix_rows, cache_rows, allowed):
    features = cache_rows.shape[1] // 2
    slots = cache_rows.shape[0]
    key_matrix_rows = cache_rows[:, :features].reshape(slots, H, HD)
    value_matrix_rows = cache_rows[:, features:].reshape(slots, H, HD)
    attention_score_scale = 1.0 / math.sqrt(HD)
    attention_scores = (
        jnp.einsum(
            "was,zas->waz", query_matrix_rows, key_matrix_rows, preferred_element_type=jnp.float32
        )
        * attention_score_scale
    )
    widened = allowed[:, None, :]
    attention_scores = jnp.where(widened, attention_scores, NEG)
    maxima = jnp.max(attention_scores, axis=-1)
    attention_weights = jnp.where(widened, jnp.exp(attention_scores - maxima[..., None]), 0.0)
    totals = jnp.sum(attention_weights, axis=-1)
    weighted_sum = jnp.einsum(
        "ubj,jbx->ubx",
        attention_weights.astype(jnp.bfloat16),
        value_matrix_rows,
        preferred_element_type=jnp.float32,
    )
    return (maxima, totals, weighted_sum)


def join_parts(first_part, second_part):
    highest = jnp.maximum(first_part[0], second_part[0])
    scale_first = jnp.exp(first_part[0] - highest)
    scale_second = jnp.exp(second_part[0] - highest)
    totals = first_part[1] * scale_first + second_part[1] * scale_second
    weighted_sum = first_part[2] * scale_first[..., None] + second_part[2] * scale_second[..., None]
    return (highest, totals, weighted_sum)


def as_rows(part_state, row_count):
    return (
        part_state[0].reshape(row_count, H),
        part_state[1].reshape(row_count, H),
        part_state[2].reshape(row_count, H, HD),
    )


def attend_kernel(*refs, count, scale):
    q_ref = refs[0]
    sources = refs[1:1 + 3 * count]
    acc_ref, top_ref, total_ref = refs[1 + 3 * count:]
    width = HD
    for head in range(q_ref.shape[1] // HD):
        cols = slice(head * width, (head + 1) * width)
        query = q_ref[:, cols]
        scores = []
        for index in range(count):
            keys = sources[3 * index][:, cols]
            raw = lax.dot_general(
                query, keys, (((1,), (1,)), ((), ())), preferred_element_type=jnp.float32
            ) * scale
            scores.append(jnp.where(sources[3 * index + 2][...] > 0.5, raw, NEG))
        top = scores[0].max(axis=1, keepdims=True)
        for more in scores[1:]:
            top = jnp.maximum(top, more.max(axis=1, keepdims=True))
        total = jnp.zeros_like(top)
        acc = jnp.zeros((query.shape[0], width), jnp.float32)
        for index in range(count):
            weights = jnp.where(sources[3 * index + 2][...] > 0.5, jnp.exp(scores[index] - top), 0.0)
            total = total + weights.sum(axis=1, keepdims=True)
            acc = acc + jnp.dot(
                weights.astype(jnp.bfloat16),
                sources[3 * index + 1][:, cols],
                preferred_element_type=jnp.float32,
            )
        acc_ref[:, cols] = acc
        top_ref[:, cols] = jnp.broadcast_to(top, acc.shape)
        total_ref[:, cols] = jnp.broadcast_to(total, acc.shape)


def attend(query_rows, sources):
    rows, features = query_rows.shape
    group = 4 if (features // HD) % 4 == 0 else 2
    pairs = features // (group * HD)
    block = group * HD
    operands = [query_rows]
    specs = [pl.BlockSpec((rows, block), lambda h: (0, h))]
    for table, key_offset, value_offset, allowed in sources:
        slots = table.shape[0]
        operands += [table, table, allowed.astype(jnp.float32)]
        specs += [
            pl.BlockSpec((slots, block), lambda h, o=key_offset: (0, o + h)),
            pl.BlockSpec((slots, block), lambda h, o=value_offset: (0, o + h)),
            pl.BlockSpec((rows, slots), lambda h: (0, 0)),
        ]
    shape = jax.ShapeDtypeStruct((rows, features), jnp.float32)
    out_spec = pl.BlockSpec((rows, block), lambda h: (0, h))
    return pl.pallas_call(
        functools.partial(attend_kernel, count=len(sources), scale=1.0 / math.sqrt(HD)),
        grid=(pairs,),
        in_specs=specs,
        out_specs=(out_spec, out_spec, out_spec),
        out_shape=(shape, shape, shape),
    )(*operands)


def expert_kernel(first_ref, second_ref, gate_ref, up_ref, down_ref, first_out, second_out, gate_acc, up_acc):
    step = pl.program_id(0)

    @pl.when(step == 0)
    def _():
        gate_acc[...] = jnp.zeros_like(gate_acc)
        up_acc[...] = jnp.zeros_like(up_acc)

    rows = jnp.concatenate([first_ref[...], second_ref[...]], axis=0)
    gate_acc[...] += jnp.dot(rows, gate_ref[...], preferred_element_type=jnp.float32)
    up_acc[...] += jnp.dot(rows, up_ref[...], preferred_element_type=jnp.float32)

    @pl.when(step == pl.num_programs(0) - 1)
    def _():
        gate_act = gate_acc[...]
        hidden_units = (gate_act / (1.0 + jnp.exp(-gate_act)) * up_acc[...]).astype(jnp.bfloat16)
        partial = jnp.dot(hidden_units, down_ref[...], preferred_element_type=jnp.float32).astype(jnp.bfloat16)
        half = first_out.shape[0]
        first_out[...] = partial[:half]
        second_out[...] = partial[half:]


def expert_block(first, second, w_gate_up, w_down):
    half, features = first.shape
    units = w_gate_up.shape[3]
    chunk = features // 3 if features % 384 == 0 else features
    steps = features // chunk
    row_spec = pl.BlockSpec((half, chunk), lambda k: (0, k))
    out_spec = pl.BlockSpec((half, features), lambda k: (0, 0))
    shape = jax.ShapeDtypeStruct((half, features), jnp.bfloat16)
    return pl.pallas_call(
        expert_kernel,
        grid=(steps,),
        in_specs=[
            row_spec,
            row_spec,
            pl.BlockSpec((None, None, chunk, units), lambda k: (0, 0, k, 0)),
            pl.BlockSpec((None, None, chunk, units), lambda k: (0, 1, k, 0)),
            pl.BlockSpec((None, units, features), lambda k: (0, 0, 0)),
        ],
        out_specs=(out_spec, out_spec),
        out_shape=(shape, shape),
        scratch_shapes=[
            pltpu.VMEM((2 * half, units), jnp.float32),
            pltpu.VMEM((2 * half, units), jnp.float32),
        ],
    )(first, second, w_gate_up, w_gate_up, w_down)


def dp_ring(mesh):
    count = mesh.shape["dp"]
    try:
        axis = list(mesh.axis_names).index("dp")
        places = [tuple(mesh.devices.take(i, axis=axis).reshape(-1)[0].coords) for i in range(count)]
        varying = [a for a in range(len(places[0])) if len({c[a] for c in places}) > 1]
        changes = {a: sum(places[i][a] != places[i + 1][a] for i in range(count - 1)) for a in varying}
        slow, fast = sorted(varying, key=lambda a: changes[a])
        rows = sorted({c[slow] for c in places})
        cols = sorted({c[fast] for c in places})
        where = {(c[slow], c[fast]): i for i, c in enumerate(places)}
        if len(varying) != 2 or len(rows) * len(cols) != count or len(rows) % 2 or len(cols) < 2:
            raise ValueError
        cycle = [where[(rows[0], cols[0])]]
        for r, row in enumerate(rows):
            ordered = cols[1:] if r % 2 == 0 else cols[1:][::-1]
            cycle += [where[(row, col)] for col in ordered]
        cycle += [where[(row, cols[0])] for row in rows[1:][::-1]]
        if sorted(cycle) != list(range(count)):
            raise ValueError
        return cycle
    except Exception:
        return list(range(count))


def ring_gather(piece, ring, step):
    count = len(ring)
    pairs = [(ring[p], ring[(p + step) % count]) for p in range(count)]
    arrived = [piece]
    for unused in range(count - 1):
        piece = lax.ppermute(piece, "dp", pairs)
        arrived.append(piece)
    return arrived


def ring_reduce(blocks, ring, step):
    count = len(ring)
    pairs = [(ring[p], ring[(p + step) % count]) for p in range(count)]
    moving = blocks[1]
    for index in range(2, count):
        received = lax.ppermute(moving, "dp", pairs).astype(jnp.float32)
        moving = (received + blocks[index].astype(jnp.float32)).astype(jnp.bfloat16)
    received = lax.ppermute(moving, "dp", pairs).astype(jnp.float32)
    return received + blocks[0].astype(jnp.float32)


def local(
    ring,
    hidden,
    tree_qkv,
    prompt_kv,
    prompt_len,
    private_kv,
    priv_len,
    parents,
    leaf,
    w_out,
    norm_gain,
    w_router,
    routes,
    w_gate_up,
    w_down,
):
    row_count = hidden.shape[0]
    features = hidden.shape[1]
    new_kv = tree_qkv[:, features:]
    reached = closure(parents)
    grouped_kv = new_kv.reshape(REQ_DEV, TREE, 2 * features)
    blocks = features // ((4 if (features // HD) % 4 == 0 else 2) * HD)
    private_slots = jnp.arange(private_kv.shape[1], dtype=jnp.int32)
    private_ok = jnp.broadcast_to(private_slots[None, :] < priv_len[0], (row_count, private_kv.shape[1]))
    local_acc, local_top, local_total = attend(
        tree_qkv[:, :features],
        [
            (private_kv[0], 0, blocks, private_ok),
            (tree_qkv, blocks, 2 * blocks, reached[0] > 0.5),
        ],
    )
    shard_rows = lax.all_gather(prompt_kv, "expert", axis=1, tiled=True)
    piece_len = shard_rows.shape[1]
    places = jnp.arange(piece_len, dtype=jnp.int32)
    prompt_ok = jnp.broadcast_to((places < prompt_len[0])[None, :], (row_count, piece_len))
    prompt_acc, prompt_top, prompt_total = attend(
        tree_qkv[:, :features], [(shard_rows[0], 0, blocks, prompt_ok)]
    )
    highest = jnp.maximum(local_top, prompt_top)
    scale_local = jnp.exp(local_top - highest)
    scale_prompt = jnp.exp(prompt_top - highest)
    totals = local_total * scale_local + prompt_total * scale_prompt
    weighted = local_acc * scale_local + prompt_acc * scale_prompt
    context = (weighted / totals).astype(jnp.bfloat16)
    attended = jnp.dot(context, w_out, preferred_element_type=jnp.float32)
    middle = (hidden.astype(jnp.float32) + attended).astype(jnp.bfloat16)
    middle32 = middle.astype(jnp.float32)
    normed = (
        middle32 * lax.rsqrt(jnp.mean(middle32 * middle32, axis=1, keepdims=True) + EPS) * norm_gain
    ).astype(jnp.bfloat16)
    logits = jnp.dot(normed, w_router, preferred_element_type=jnp.float32)
    experts = w_router.shape[1]
    choose = routes[:, :, None] == jnp.arange(experts, dtype=jnp.int32)[None, None, :]
    picked = jnp.sum(jnp.where(choose, logits[:, None, :], 0.0), axis=2)
    gate_first = jax.nn.sigmoid(picked[:, 0] - picked[:, 1])
    gate_second = jax.nn.sigmoid(picked[:, 1] - picked[:, 0])
    capacity = 3 * row_count // experts
    onehot = choose.reshape(2 * row_count, experts).astype(jnp.float32)
    assign_ids = jnp.arange(2 * row_count, dtype=jnp.int32)
    earlier = (assign_ids[None, :] < assign_ids[:, None]).astype(jnp.float32)
    before = jnp.dot(earlier, onehot, precision=HIGH)
    slot_rank = jnp.sum(before * onehot, axis=1).astype(jnp.int32)
    target = routes.reshape(2 * row_count) * capacity + slot_rank
    select = (jnp.arange(experts * capacity, dtype=jnp.int32)[:, None] == target[None, :]).astype(
        jnp.bfloat16
    )
    doubled = jnp.repeat(normed, 2, axis=0)
    outgoing = (
        jnp.dot(select, doubled, preferred_element_type=jnp.float32)
        .astype(jnp.bfloat16)
        .reshape(experts, capacity, features)
    )
    gate_cols = w_gate_up[0, 0]
    up_cols = w_gate_up[0, 1]
    down_rows = w_down[0]
    arrived = lax.all_to_all(outgoing, "expert", split_axis=0, concat_axis=0, tiled=True)
    arrived = arrived.reshape(experts * capacity, features)
    half = experts * capacity // 2
    forward = ring_gather(arrived[:half], ring, 1)
    backward = ring_gather(arrived[half:], ring, -1)
    forward_out = []
    backward_out = []
    for index in range(len(ring)):
        first_part, second_part = expert_block(forward[index], backward[index], w_gate_up, w_down)
        forward_out.append(first_part)
        backward_out.append(second_part)
    summed_rows = jnp.concatenate(
        [ring_reduce(forward_out, ring, 1), ring_reduce(backward_out, ring, -1)], axis=0
    )
    returned = lax.all_to_all(
        summed_rows.reshape(experts, capacity, features).astype(jnp.bfloat16),
        "expert",
        split_axis=0,
        concat_axis=0,
        tiled=True,
    ).astype(jnp.float32)
    flat_back = returned.reshape(experts * capacity, features)
    fetched = jnp.take(flat_back, target, axis=0).reshape(row_count, 2, features)
    layer_out = (
        middle32 + gate_first[:, None] * fetched[:, 0] + gate_second[:, None] * fetched[:, 1]
    ).astype(jnp.bfloat16)
    accepted_kv = jax.vmap(compact)(reached, leaf, grouped_kv)
    return (layer_out, accepted_kv)


def solution(mesh):
    placed = (
        P(("dp", "expert"), None),
        P(("dp", "expert"), None),
        P("dp", "expert", None),
        P("dp"),
        P(("dp", "expert"), None, None),
        P(("dp", "expert")),
        P(("dp", "expert"), None),
        P(("dp", "expert")),
        P(),
        P(),
        P(),
        P(("dp", "expert"), None),
        P("expert", None, None, "dp"),
        P("expert", "dp", None),
    )
    ring = dp_ring(mesh)
    return jax.shard_map(
        functools.partial(local, ring),
        mesh=mesh,
        in_specs=placed,
        out_specs=(P(("dp", "expert"), None), P(("dp", "expert"), None, None)),
        check_vma=False,
    )
```

```python
import functools
import math

import jax
import jax.numpy as jnp
from jax import lax
from jax.experimental import pallas as pl
from jax.sharding import PartitionSpec as P

H = 36
HD = 64
TREE = 64
REQ_DEV = 1


NEG = -1e30
EPS = 1e-05
HIGH = lax.Precision.HIGHEST


def closure(parents):
    count = parents.shape[-1]
    columns = jnp.arange(count, dtype=jnp.int32)
    reached = (parents[:, :, None] == columns[None, None, :]).astype(jnp.float32) + jnp.eye(
        count, dtype=jnp.float32
    )[None]
    for sweeps in range((count - 1).bit_length()):
        reached = jnp.minimum(jnp.einsum("rij,rjk->rik", reached, reached, precision=HIGH), 1.0)
    return reached


def compact(reach_one, leaf_one, kv_one):
    count = reach_one.shape[0]
    marked = jnp.sum(
        jnp.where(jnp.arange(count, dtype=jnp.int32)[:, None] == leaf_one, reach_one, 0.0), axis=0
    )
    earlier = (
        jnp.arange(count, dtype=jnp.int32)[None, :] < jnp.arange(count, dtype=jnp.int32)[:, None]
    ).astype(jnp.float32)
    ordinal = jnp.dot(earlier, marked, precision=HIGH)
    slot_ids = jnp.arange(count, dtype=jnp.int32).astype(jnp.float32)
    chosen = jnp.where(slot_ids[:, None] == ordinal[None, :], marked[None, :], 0.0)
    return jnp.dot(chosen.astype(jnp.bfloat16), kv_one, preferred_element_type=jnp.float32).astype(
        jnp.bfloat16
    )


def partial_attention(query_matrix_rows, cache_rows, allowed):
    features = cache_rows.shape[1] // 2
    slots = cache_rows.shape[0]
    key_matrix_rows = cache_rows[:, :features].reshape(slots, H, HD)
    value_matrix_rows = cache_rows[:, features:].reshape(slots, H, HD)
    attention_score_scale = 1.0 / math.sqrt(HD)
    attention_scores = (
        jnp.einsum(
            "was,zas->waz", query_matrix_rows, key_matrix_rows, preferred_element_type=jnp.float32
        )
        * attention_score_scale
    )
    widened = allowed[:, None, :]
    attention_scores = jnp.where(widened, attention_scores, NEG)
    maxima = jnp.max(attention_scores, axis=-1)
    attention_weights = jnp.where(widened, jnp.exp(attention_scores - maxima[..., None]), 0.0)
    totals = jnp.sum(attention_weights, axis=-1)
    weighted_sum = jnp.einsum(
        "ubj,jbx->ubx",
        attention_weights.astype(jnp.bfloat16),
        value_matrix_rows,
        preferred_element_type=jnp.float32,
    )
    return (maxima, totals, weighted_sum)


def join_parts(first_part, second_part):
    highest = jnp.maximum(first_part[0], second_part[0])
    scale_first = jnp.exp(first_part[0] - highest)
    scale_second = jnp.exp(second_part[0] - highest)
    totals = first_part[1] * scale_first + second_part[1] * scale_second
    weighted_sum = first_part[2] * scale_first[..., None] + second_part[2] * scale_second[..., None]
    return (highest, totals, weighted_sum)


def as_rows(part_state, row_count):
    return (
        part_state[0].reshape(row_count, H),
        part_state[1].reshape(row_count, H),
        part_state[2].reshape(row_count, H, HD),
    )


def attend_kernel(*refs, count, scale):
    q_ref = refs[0]
    sources = refs[1:1 + 3 * count]
    acc_ref, top_ref, total_ref = refs[1 + 3 * count:]
    width = HD
    for head in range(q_ref.shape[1] // HD):
        cols = slice(head * width, (head + 1) * width)
        query = q_ref[:, cols]
        scores = []
        for index in range(count):
            keys = sources[3 * index][:, cols]
            raw = lax.dot_general(
                query, keys, (((1,), (1,)), ((), ())), preferred_element_type=jnp.float32
            ) * scale
            scores.append(jnp.where(sources[3 * index + 2][...] > 0.5, raw, NEG))
        top = scores[0].max(axis=1, keepdims=True)
        for more in scores[1:]:
            top = jnp.maximum(top, more.max(axis=1, keepdims=True))
        total = jnp.zeros_like(top)
        acc = jnp.zeros((query.shape[0], width), jnp.float32)
        for index in range(count):
            weights = jnp.where(sources[3 * index + 2][...] > 0.5, jnp.exp(scores[index] - top), 0.0)
            total = total + weights.sum(axis=1, keepdims=True)
            acc = acc + jnp.dot(
                weights.astype(jnp.bfloat16),
                sources[3 * index + 1][:, cols],
                preferred_element_type=jnp.float32,
            )
        acc_ref[:, cols] = acc
        top_ref[:, cols] = jnp.broadcast_to(top, acc.shape)
        total_ref[:, cols] = jnp.broadcast_to(total, acc.shape)


def attend(query_rows, sources):
    rows, features = query_rows.shape
    group = 4 if (features // HD) % 4 == 0 else 2
    pairs = features // (group * HD)
    block = group * HD
    operands = [query_rows]
    specs = [pl.BlockSpec((rows, block), lambda h: (0, h))]
    for table, key_offset, value_offset, allowed in sources:
        slots = table.shape[0]
        operands += [table, table, allowed.astype(jnp.float32)]
        specs += [
            pl.BlockSpec((slots, block), lambda h, o=key_offset: (0, o + h)),
            pl.BlockSpec((slots, block), lambda h, o=value_offset: (0, o + h)),
            pl.BlockSpec((rows, slots), lambda h: (0, 0)),
        ]
    shape = jax.ShapeDtypeStruct((rows, features), jnp.float32)
    out_spec = pl.BlockSpec((rows, block), lambda h: (0, h))
    return pl.pallas_call(
        functools.partial(attend_kernel, count=len(sources), scale=1.0 / math.sqrt(HD)),
        grid=(pairs,),
        in_specs=specs,
        out_specs=(out_spec, out_spec, out_spec),
        out_shape=(shape, shape, shape),
    )(*operands)


def dp_ring(mesh):
    count = mesh.shape["dp"]
    try:
        axis = list(mesh.axis_names).index("dp")
        places = [tuple(mesh.devices.take(i, axis=axis).reshape(-1)[0].coords) for i in range(count)]
        varying = [a for a in range(len(places[0])) if len({c[a] for c in places}) > 1]
        changes = {a: sum(places[i][a] != places[i + 1][a] for i in range(count - 1)) for a in varying}
        slow, fast = sorted(varying, key=lambda a: changes[a])
        rows = sorted({c[slow] for c in places})
        cols = sorted({c[fast] for c in places})
        where = {(c[slow], c[fast]): i for i, c in enumerate(places)}
        if len(varying) != 2 or len(rows) * len(cols) != count or len(rows) % 2 or len(cols) < 2:
            raise ValueError
        cycle = [where[(rows[0], cols[0])]]
        for r, row in enumerate(rows):
            ordered = cols[1:] if r % 2 == 0 else cols[1:][::-1]
            cycle += [where[(row, col)] for col in ordered]
        cycle += [where[(row, cols[0])] for row in rows[1:][::-1]]
        if sorted(cycle) != list(range(count)):
            raise ValueError
        return cycle
    except Exception:
        return list(range(count))


def ring_gather(piece, ring, step):
    count = len(ring)
    pairs = [(ring[p], ring[(p + step) % count]) for p in range(count)]
    arrived = [piece]
    for unused in range(count - 1):
        piece = lax.ppermute(piece, "dp", pairs)
        arrived.append(piece)
    return arrived


def ring_reduce(blocks, ring, step):
    count = len(ring)
    pairs = [(ring[p], ring[(p + step) % count]) for p in range(count)]
    moving = blocks[1]
    for index in range(2, count):
        received = lax.ppermute(moving, "dp", pairs).astype(jnp.float32)
        moving = (received + blocks[index].astype(jnp.float32)).astype(jnp.bfloat16)
    received = lax.ppermute(moving, "dp", pairs).astype(jnp.float32)
    return received + blocks[0].astype(jnp.float32)


def local(
    ring,
    hidden,
    tree_qkv,
    prompt_kv,
    prompt_len,
    private_kv,
    priv_len,
    parents,
    leaf,
    w_out,
    norm_gain,
    w_router,
    routes,
    w_gate_up,
    w_down,
):
    row_count = hidden.shape[0]
    features = hidden.shape[1]
    new_kv = tree_qkv[:, features:]
    reached = closure(parents)
    grouped_kv = new_kv.reshape(REQ_DEV, TREE, 2 * features)
    blocks = features // ((4 if (features // HD) % 4 == 0 else 2) * HD)
    private_slots = jnp.arange(private_kv.shape[1], dtype=jnp.int32)
    private_ok = jnp.broadcast_to(private_slots[None, :] < priv_len[0], (row_count, private_kv.shape[1]))
    local_acc, local_top, local_total = attend(
        tree_qkv[:, :features],
        [
            (private_kv[0], 0, blocks, private_ok),
            (tree_qkv, blocks, 2 * blocks, reached[0] > 0.5),
        ],
    )
    shard_rows = lax.all_gather(prompt_kv, "expert", axis=1, tiled=True)
    piece_len = shard_rows.shape[1]
    places = jnp.arange(piece_len, dtype=jnp.int32)
    prompt_ok = jnp.broadcast_to((places < prompt_len[0])[None, :], (row_count, piece_len))
    prompt_acc, prompt_top, prompt_total = attend(
        tree_qkv[:, :features], [(shard_rows[0], 0, blocks, prompt_ok)]
    )
    highest = jnp.maximum(local_top, prompt_top)
    scale_local = jnp.exp(local_top - highest)
    scale_prompt = jnp.exp(prompt_top - highest)
    totals = local_total * scale_local + prompt_total * scale_prompt
    weighted = local_acc * scale_local + prompt_acc * scale_prompt
    context = (weighted / totals).astype(jnp.bfloat16)
    attended = jnp.dot(context, w_out, preferred_element_type=jnp.float32)
    middle = (hidden.astype(jnp.float32) + attended).astype(jnp.bfloat16)
    middle32 = middle.astype(jnp.float32)
    normed = (
        middle32 * lax.rsqrt(jnp.mean(middle32 * middle32, axis=1, keepdims=True) + EPS) * norm_gain
    ).astype(jnp.bfloat16)
    logits = jnp.dot(normed, w_router, preferred_element_type=jnp.float32)
    experts = w_router.shape[1]
    choose = routes[:, :, None] == jnp.arange(experts, dtype=jnp.int32)[None, None, :]
    picked = jnp.sum(jnp.where(choose, logits[:, None, :], 0.0), axis=2)
    gate_first = jax.nn.sigmoid(picked[:, 0] - picked[:, 1])
    gate_second = jax.nn.sigmoid(picked[:, 1] - picked[:, 0])
    capacity = 3 * row_count // experts
    onehot = choose.reshape(2 * row_count, experts).astype(jnp.float32)
    assign_ids = jnp.arange(2 * row_count, dtype=jnp.int32)
    earlier = (assign_ids[None, :] < assign_ids[:, None]).astype(jnp.float32)
    before = jnp.dot(earlier, onehot, precision=HIGH)
    slot_rank = jnp.sum(before * onehot, axis=1).astype(jnp.int32)
    target = routes.reshape(2 * row_count) * capacity + slot_rank
    select = (jnp.arange(experts * capacity, dtype=jnp.int32)[:, None] == target[None, :]).astype(
        jnp.bfloat16
    )
    doubled = jnp.repeat(normed, 2, axis=0)
    outgoing = (
        jnp.dot(select, doubled, preferred_element_type=jnp.float32)
        .astype(jnp.bfloat16)
        .reshape(experts, capacity, features)
    )
    gate_cols = w_gate_up[0, 0]
    up_cols = w_gate_up[0, 1]
    down_rows = w_down[0]
    split = capacity // 2
    half = experts * split
    first_rows = lax.all_to_all(outgoing[:, :split], "expert", split_axis=0, concat_axis=0, tiled=True)
    second_rows = lax.all_to_all(outgoing[:, split:], "expert", split_axis=0, concat_axis=0, tiled=True)
    forward = ring_gather(first_rows.reshape(half, features), ring, 1)
    backward = ring_gather(second_rows.reshape(half, features), ring, -1)
    forward_out = []
    backward_out = []
    for index in range(len(ring)):
        pooled = jnp.concatenate([forward[index], backward[index]], axis=0)
        gate_act = jnp.dot(pooled, gate_cols, preferred_element_type=jnp.float32)
        upper = jnp.dot(pooled, up_cols, preferred_element_type=jnp.float32)
        hidden_units = (jax.nn.silu(gate_act) * upper).astype(jnp.bfloat16)
        partial = jnp.dot(hidden_units, down_rows, preferred_element_type=jnp.float32).astype(jnp.bfloat16)
        forward_out.append(partial[:half])
        backward_out.append(partial[half:])
    first_back = lax.all_to_all(
        ring_reduce(forward_out, ring, 1).astype(jnp.bfloat16).reshape(experts, split, features),
        "expert",
        split_axis=0,
        concat_axis=0,
        tiled=True,
    )
    second_back = lax.all_to_all(
        ring_reduce(backward_out, ring, -1).astype(jnp.bfloat16).reshape(experts, split, features),
        "expert",
        split_axis=0,
        concat_axis=0,
        tiled=True,
    )
    flat_back = jnp.concatenate([first_back, second_back], axis=1).reshape(experts * capacity, features)
    pick = (target[:, None] == jnp.arange(experts * capacity, dtype=jnp.int32)[None, :]).astype(jnp.bfloat16)
    fetched = jnp.dot(pick, flat_back, preferred_element_type=jnp.float32).reshape(row_count, 2, features)
    layer_out = (
        middle32 + gate_first[:, None] * fetched[:, 0] + gate_second[:, None] * fetched[:, 1]
    ).astype(jnp.bfloat16)
    accepted_kv = jax.vmap(compact)(reached, leaf, grouped_kv)
    return (layer_out, accepted_kv)


def solution(mesh):
    placed = (
        P(("dp", "expert"), None),
        P(("dp", "expert"), None),
        P("dp", "expert", None),
        P("dp"),
        P(("dp", "expert"), None, None),
        P(("dp", "expert")),
        P(("dp", "expert"), None),
        P(("dp", "expert")),
        P(),
        P(),
        P(),
        P(("dp", "expert"), None),
        P("expert", None, None, "dp"),
        P("expert", "dp", None),
    )
    ring = dp_ring(mesh)
    return jax.shard_map(
        functools.partial(local, ring),
        mesh=mesh,
        in_specs=placed,
        out_specs=(P(("dp", "expert"), None), P(("dp", "expert"), None, None)),
        check_vma=False,
    )
```

```python
import functools
import math

import jax
import jax.numpy as jnp
from jax import lax
from jax.experimental import pallas as pl
from jax.sharding import PartitionSpec as P

H = 36
HD = 64
TREE = 64
REQ_DEV = 1


NEG = -1e30
EPS = 1e-05
HIGH = lax.Precision.HIGHEST


def closure(parents):
    count = parents.shape[-1]
    columns = jnp.arange(count, dtype=jnp.int32)
    reached = (parents[:, :, None] == columns[None, None, :]).astype(jnp.float32) + jnp.eye(
        count, dtype=jnp.float32
    )[None]
    for sweeps in range((count - 1).bit_length()):
        reached = jnp.minimum(jnp.einsum("rij,rjk->rik", reached, reached, precision=HIGH), 1.0)
    return reached


def compact(reach_one, leaf_one, kv_one):
    count = reach_one.shape[0]
    marked = jnp.sum(
        jnp.where(jnp.arange(count, dtype=jnp.int32)[:, None] == leaf_one, reach_one, 0.0), axis=0
    )
    earlier = (
        jnp.arange(count, dtype=jnp.int32)[None, :] < jnp.arange(count, dtype=jnp.int32)[:, None]
    ).astype(jnp.float32)
    ordinal = jnp.dot(earlier, marked, precision=HIGH)
    slot_ids = jnp.arange(count, dtype=jnp.int32).astype(jnp.float32)
    chosen = jnp.where(slot_ids[:, None] == ordinal[None, :], marked[None, :], 0.0)
    return jnp.dot(chosen.astype(jnp.bfloat16), kv_one, preferred_element_type=jnp.float32).astype(
        jnp.bfloat16
    )


def partial_attention(query_matrix_rows, cache_rows, allowed):
    features = cache_rows.shape[1] // 2
    slots = cache_rows.shape[0]
    key_matrix_rows = cache_rows[:, :features].reshape(slots, H, HD)
    value_matrix_rows = cache_rows[:, features:].reshape(slots, H, HD)
    attention_score_scale = 1.0 / math.sqrt(HD)
    attention_scores = (
        jnp.einsum(
            "was,zas->waz", query_matrix_rows, key_matrix_rows, preferred_element_type=jnp.float32
        )
        * attention_score_scale
    )
    widened = allowed[:, None, :]
    attention_scores = jnp.where(widened, attention_scores, NEG)
    maxima = jnp.max(attention_scores, axis=-1)
    attention_weights = jnp.where(widened, jnp.exp(attention_scores - maxima[..., None]), 0.0)
    totals = jnp.sum(attention_weights, axis=-1)
    weighted_sum = jnp.einsum(
        "ubj,jbx->ubx",
        attention_weights.astype(jnp.bfloat16),
        value_matrix_rows,
        preferred_element_type=jnp.float32,
    )
    return (maxima, totals, weighted_sum)


def join_parts(first_part, second_part):
    highest = jnp.maximum(first_part[0], second_part[0])
    scale_first = jnp.exp(first_part[0] - highest)
    scale_second = jnp.exp(second_part[0] - highest)
    totals = first_part[1] * scale_first + second_part[1] * scale_second
    weighted_sum = first_part[2] * scale_first[..., None] + second_part[2] * scale_second[..., None]
    return (highest, totals, weighted_sum)


def as_rows(part_state, row_count):
    return (
        part_state[0].reshape(row_count, H),
        part_state[1].reshape(row_count, H),
        part_state[2].reshape(row_count, H, HD),
    )


def attend_kernel(*refs, count, scale):
    q_ref = refs[0]
    sources = refs[1:1 + 3 * count]
    acc_ref, top_ref, total_ref = refs[1 + 3 * count:]
    width = HD
    for head in range(q_ref.shape[1] // HD):
        cols = slice(head * width, (head + 1) * width)
        query = q_ref[:, cols]
        scores = []
        for index in range(count):
            keys = sources[3 * index][:, cols]
            raw = lax.dot_general(
                query, keys, (((1,), (1,)), ((), ())), preferred_element_type=jnp.float32
            ) * scale
            scores.append(jnp.where(sources[3 * index + 2][...] > 0.5, raw, NEG))
        top = scores[0].max(axis=1, keepdims=True)
        for more in scores[1:]:
            top = jnp.maximum(top, more.max(axis=1, keepdims=True))
        total = jnp.zeros_like(top)
        acc = jnp.zeros((query.shape[0], width), jnp.float32)
        for index in range(count):
            weights = jnp.where(sources[3 * index + 2][...] > 0.5, jnp.exp(scores[index] - top), 0.0)
            total = total + weights.sum(axis=1, keepdims=True)
            acc = acc + jnp.dot(
                weights.astype(jnp.bfloat16),
                sources[3 * index + 1][:, cols],
                preferred_element_type=jnp.float32,
            )
        acc_ref[:, cols] = acc
        top_ref[:, cols] = jnp.broadcast_to(top, acc.shape)
        total_ref[:, cols] = jnp.broadcast_to(total, acc.shape)


def attend(query_rows, sources):
    rows, features = query_rows.shape
    group = 4 if (features // HD) % 4 == 0 else 2
    pairs = features // (group * HD)
    block = group * HD
    operands = [query_rows]
    specs = [pl.BlockSpec((rows, block), lambda h: (0, h))]
    for table, key_offset, value_offset, allowed in sources:
        slots = table.shape[0]
        operands += [table, table, allowed.astype(jnp.float32)]
        specs += [
            pl.BlockSpec((slots, block), lambda h, o=key_offset: (0, o + h)),
            pl.BlockSpec((slots, block), lambda h, o=value_offset: (0, o + h)),
            pl.BlockSpec((rows, slots), lambda h: (0, 0)),
        ]
    shape = jax.ShapeDtypeStruct((rows, features), jnp.float32)
    out_spec = pl.BlockSpec((rows, block), lambda h: (0, h))
    return pl.pallas_call(
        functools.partial(attend_kernel, count=len(sources), scale=1.0 / math.sqrt(HD)),
        grid=(pairs,),
        in_specs=specs,
        out_specs=(out_spec, out_spec, out_spec),
        out_shape=(shape, shape, shape),
    )(*operands)


def dp_ring(mesh):
    count = mesh.shape["dp"]
    try:
        axis = list(mesh.axis_names).index("dp")
        places = [tuple(mesh.devices.take(i, axis=axis).reshape(-1)[0].coords) for i in range(count)]
        varying = [a for a in range(len(places[0])) if len({c[a] for c in places}) > 1]
        changes = {a: sum(places[i][a] != places[i + 1][a] for i in range(count - 1)) for a in varying}
        slow, fast = sorted(varying, key=lambda a: changes[a])
        rows = sorted({c[slow] for c in places})
        cols = sorted({c[fast] for c in places})
        where = {(c[slow], c[fast]): i for i, c in enumerate(places)}
        if len(varying) != 2 or len(rows) * len(cols) != count or len(rows) % 2 or len(cols) < 2:
            raise ValueError
        cycle = [where[(rows[0], cols[0])]]
        for r, row in enumerate(rows):
            ordered = cols[1:] if r % 2 == 0 else cols[1:][::-1]
            cycle += [where[(row, col)] for col in ordered]
        cycle += [where[(row, cols[0])] for row in rows[1:][::-1]]
        if sorted(cycle) != list(range(count)):
            raise ValueError
        return cycle
    except Exception:
        return list(range(count))


def ring_gather(piece, ring, step):
    count = len(ring)
    pairs = [(ring[p], ring[(p + step) % count]) for p in range(count)]
    arrived = [piece]
    for unused in range(count - 1):
        piece = lax.ppermute(piece, "dp", pairs)
        arrived.append(piece)
    return arrived


def ring_reduce(blocks, ring, step):
    count = len(ring)
    pairs = [(ring[p], ring[(p + step) % count]) for p in range(count)]
    moving = blocks[1]
    for index in range(2, count):
        received = lax.ppermute(moving, "dp", pairs).astype(jnp.float32)
        moving = (received + blocks[index].astype(jnp.float32)).astype(jnp.bfloat16)
    received = lax.ppermute(moving, "dp", pairs).astype(jnp.float32)
    return received + blocks[0].astype(jnp.float32)


def local(
    ring,
    hidden,
    tree_qkv,
    prompt_kv,
    prompt_len,
    private_kv,
    priv_len,
    parents,
    leaf,
    w_out,
    norm_gain,
    w_router,
    routes,
    w_gate_up,
    w_down,
):
    row_count = hidden.shape[0]
    features = hidden.shape[1]
    new_kv = tree_qkv[:, features:]
    reached = closure(parents)
    grouped_kv = new_kv.reshape(REQ_DEV, TREE, 2 * features)
    blocks = features // ((4 if (features // HD) % 4 == 0 else 2) * HD)
    private_slots = jnp.arange(private_kv.shape[1], dtype=jnp.int32)
    private_ok = jnp.broadcast_to(private_slots[None, :] < priv_len[0], (row_count, private_kv.shape[1]))
    local_acc, local_top, local_total = attend(
        tree_qkv[:, :features],
        [
            (private_kv[0], 0, blocks, private_ok),
            (tree_qkv, blocks, 2 * blocks, reached[0] > 0.5),
        ],
    )
    shard_rows = lax.all_gather(prompt_kv, "expert", axis=1, tiled=True)
    piece_len = shard_rows.shape[1]
    places = jnp.arange(piece_len, dtype=jnp.int32)
    prompt_ok = jnp.broadcast_to((places < prompt_len[0])[None, :], (row_count, piece_len))
    prompt_acc, prompt_top, prompt_total = attend(
        tree_qkv[:, :features], [(shard_rows[0], 0, blocks, prompt_ok)]
    )
    highest = jnp.maximum(local_top, prompt_top)
    scale_local = jnp.exp(local_top - highest)
    scale_prompt = jnp.exp(prompt_top - highest)
    totals = local_total * scale_local + prompt_total * scale_prompt
    weighted = local_acc * scale_local + prompt_acc * scale_prompt
    context = (weighted / totals).astype(jnp.bfloat16)
    attended = jnp.dot(context, w_out, preferred_element_type=jnp.float32)
    middle = (hidden.astype(jnp.float32) + attended).astype(jnp.bfloat16)
    middle32 = middle.astype(jnp.float32)
    normed = (
        middle32 * lax.rsqrt(jnp.mean(middle32 * middle32, axis=1, keepdims=True) + EPS) * norm_gain
    ).astype(jnp.bfloat16)
    logits = jnp.dot(normed, w_router, preferred_element_type=jnp.float32)
    experts = w_router.shape[1]
    choose = routes[:, :, None] == jnp.arange(experts, dtype=jnp.int32)[None, None, :]
    picked = jnp.sum(jnp.where(choose, logits[:, None, :], 0.0), axis=2)
    gate_first = jax.nn.sigmoid(picked[:, 0] - picked[:, 1])
    gate_second = jax.nn.sigmoid(picked[:, 1] - picked[:, 0])
    capacity = 3 * row_count // experts
    onehot = choose.reshape(2 * row_count, experts).astype(jnp.float32)
    assign_ids = jnp.arange(2 * row_count, dtype=jnp.int32)
    earlier = (assign_ids[None, :] < assign_ids[:, None]).astype(jnp.float32)
    before = jnp.dot(earlier, onehot, precision=HIGH)
    slot_rank = jnp.sum(before * onehot, axis=1).astype(jnp.int32)
    own = lax.axis_index("expert")
    shift_of = (routes.reshape(2 * row_count) - own) % experts
    target = shift_of * capacity + slot_rank
    select = (jnp.arange(experts * capacity, dtype=jnp.int32)[:, None] == target[None, :]).astype(
        jnp.bfloat16
    )
    doubled = jnp.repeat(normed, 2, axis=0)
    outgoing = (
        jnp.dot(select, doubled, preferred_element_type=jnp.float32)
        .astype(jnp.bfloat16)
        .reshape(experts, capacity, features)
    )
    gate_cols = w_gate_up[0, 0]
    up_cols = w_gate_up[0, 1]
    down_rows = w_down[0]
    def shifted(rows, shift):
        if shift % experts == 0:
            return rows
        return lax.ppermute(rows, "expert", [(j, (j + shift) % experts) for j in range(experts)])

    arrived = [shifted(outgoing[shift], shift) for shift in range(experts)]
    half = experts * capacity // 2
    forward = ring_gather(jnp.concatenate(arrived[: experts // 2], axis=0), ring, 1)
    backward = ring_gather(jnp.concatenate(arrived[experts // 2 :], axis=0), ring, -1)
    forward_out = []
    backward_out = []
    for index in range(len(ring)):
        pooled = jnp.concatenate([forward[index], backward[index]], axis=0)
        gate_act = jnp.dot(pooled, gate_cols, preferred_element_type=jnp.float32)
        upper = jnp.dot(pooled, up_cols, preferred_element_type=jnp.float32)
        hidden_units = (jax.nn.silu(gate_act) * upper).astype(jnp.bfloat16)
        partial = jnp.dot(hidden_units, down_rows, preferred_element_type=jnp.float32).astype(jnp.bfloat16)
        forward_out.append(partial[:half])
        backward_out.append(partial[half:])
    summed_rows = jnp.concatenate(
        [ring_reduce(forward_out, ring, 1), ring_reduce(backward_out, ring, -1)], axis=0
    ).astype(jnp.bfloat16).reshape(experts, capacity, features)
    flat_back = jnp.concatenate(
        [shifted(summed_rows[shift], -shift) for shift in range(experts)], axis=0
    )
    pick = (target[:, None] == jnp.arange(experts * capacity, dtype=jnp.int32)[None, :]).astype(jnp.bfloat16)
    fetched = jnp.dot(pick, flat_back, preferred_element_type=jnp.float32).reshape(row_count, 2, features)
    layer_out = (
        middle32 + gate_first[:, None] * fetched[:, 0] + gate_second[:, None] * fetched[:, 1]
    ).astype(jnp.bfloat16)
    accepted_kv = jax.vmap(compact)(reached, leaf, grouped_kv)
    return (layer_out, accepted_kv)


def solution(mesh):
    placed = (
        P(("dp", "expert"), None),
        P(("dp", "expert"), None),
        P("dp", "expert", None),
        P("dp"),
        P(("dp", "expert"), None, None),
        P(("dp", "expert")),
        P(("dp", "expert"), None),
        P(("dp", "expert")),
        P(),
        P(),
        P(),
        P(("dp", "expert"), None),
        P("expert", None, None, "dp"),
        P("expert", "dp", None),
    )
    ring = dp_ring(mesh)
    return jax.shard_map(
        functools.partial(local, ring),
        mesh=mesh,
        in_specs=placed,
        out_specs=(P(("dp", "expert"), None), P(("dp", "expert"), None, None)),
        check_vma=False,
    )
```

```python
import functools
import math

import jax
import jax.numpy as jnp
from jax import lax
from jax.experimental import pallas as pl
from jax.sharding import PartitionSpec as P

H = 36
HD = 64
TREE = 64
REQ_DEV = 1


NEG = -1e30
EPS = 1e-05
HIGH = lax.Precision.HIGHEST


def closure(parents):
    count = parents.shape[-1]
    columns = jnp.arange(count, dtype=jnp.int32)
    reached = (parents[:, :, None] == columns[None, None, :]).astype(jnp.float32) + jnp.eye(
        count, dtype=jnp.float32
    )[None]
    for sweeps in range((count - 1).bit_length()):
        reached = jnp.minimum(jnp.einsum("rij,rjk->rik", reached, reached, precision=HIGH), 1.0)
    return reached


def compact(reach_one, leaf_one, kv_one):
    count = reach_one.shape[0]
    marked = jnp.sum(
        jnp.where(jnp.arange(count, dtype=jnp.int32)[:, None] == leaf_one, reach_one, 0.0), axis=0
    )
    earlier = (
        jnp.arange(count, dtype=jnp.int32)[None, :] < jnp.arange(count, dtype=jnp.int32)[:, None]
    ).astype(jnp.float32)
    ordinal = jnp.dot(earlier, marked, precision=HIGH)
    slot_ids = jnp.arange(count, dtype=jnp.int32).astype(jnp.float32)
    chosen = jnp.where(slot_ids[:, None] == ordinal[None, :], marked[None, :], 0.0)
    return jnp.dot(chosen.astype(jnp.bfloat16), kv_one, preferred_element_type=jnp.float32).astype(
        jnp.bfloat16
    )


def partial_attention(query_matrix_rows, cache_rows, allowed):
    features = cache_rows.shape[1] // 2
    slots = cache_rows.shape[0]
    key_matrix_rows = cache_rows[:, :features].reshape(slots, H, HD)
    value_matrix_rows = cache_rows[:, features:].reshape(slots, H, HD)
    attention_score_scale = 1.0 / math.sqrt(HD)
    attention_scores = (
        jnp.einsum(
            "was,zas->waz", query_matrix_rows, key_matrix_rows, preferred_element_type=jnp.float32
        )
        * attention_score_scale
    )
    widened = allowed[:, None, :]
    attention_scores = jnp.where(widened, attention_scores, NEG)
    maxima = jnp.max(attention_scores, axis=-1)
    attention_weights = jnp.where(widened, jnp.exp(attention_scores - maxima[..., None]), 0.0)
    totals = jnp.sum(attention_weights, axis=-1)
    weighted_sum = jnp.einsum(
        "ubj,jbx->ubx",
        attention_weights.astype(jnp.bfloat16),
        value_matrix_rows,
        preferred_element_type=jnp.float32,
    )
    return (maxima, totals, weighted_sum)


def join_parts(first_part, second_part):
    highest = jnp.maximum(first_part[0], second_part[0])
    scale_first = jnp.exp(first_part[0] - highest)
    scale_second = jnp.exp(second_part[0] - highest)
    totals = first_part[1] * scale_first + second_part[1] * scale_second
    weighted_sum = first_part[2] * scale_first[..., None] + second_part[2] * scale_second[..., None]
    return (highest, totals, weighted_sum)


def as_rows(part_state, row_count):
    return (
        part_state[0].reshape(row_count, H),
        part_state[1].reshape(row_count, H),
        part_state[2].reshape(row_count, H, HD),
    )


def attend_kernel(*refs, count, scale):
    q_ref = refs[0]
    sources = refs[1:1 + 3 * count]
    acc_ref, top_ref, total_ref = refs[1 + 3 * count:]
    width = HD
    for head in range(q_ref.shape[1] // HD):
        cols = slice(head * width, (head + 1) * width)
        query = q_ref[:, cols]
        scores = []
        for index in range(count):
            keys = sources[3 * index][:, cols]
            raw = lax.dot_general(
                query, keys, (((1,), (1,)), ((), ())), preferred_element_type=jnp.float32
            ) * scale
            scores.append(jnp.where(sources[3 * index + 2][...] > 0.5, raw, NEG))
        top = scores[0].max(axis=1, keepdims=True)
        for more in scores[1:]:
            top = jnp.maximum(top, more.max(axis=1, keepdims=True))
        total = jnp.zeros_like(top)
        acc = jnp.zeros((query.shape[0], width), jnp.float32)
        for index in range(count):
            weights = jnp.where(sources[3 * index + 2][...] > 0.5, jnp.exp(scores[index] - top), 0.0)
            total = total + weights.sum(axis=1, keepdims=True)
            acc = acc + jnp.dot(
                weights.astype(jnp.bfloat16),
                sources[3 * index + 1][:, cols],
                preferred_element_type=jnp.float32,
            )
        acc_ref[:, cols] = acc
        top_ref[:, cols] = jnp.broadcast_to(top, acc.shape)
        total_ref[:, cols] = jnp.broadcast_to(total, acc.shape)


def attend(query_rows, sources):
    rows, features = query_rows.shape
    group = 4 if (features // HD) % 4 == 0 else 2
    pairs = features // (group * HD)
    block = group * HD
    operands = [query_rows]
    specs = [pl.BlockSpec((rows, block), lambda h: (0, h))]
    for table, key_offset, value_offset, allowed in sources:
        slots = table.shape[0]
        operands += [table, table, allowed.astype(jnp.float32)]
        specs += [
            pl.BlockSpec((slots, block), lambda h, o=key_offset: (0, o + h)),
            pl.BlockSpec((slots, block), lambda h, o=value_offset: (0, o + h)),
            pl.BlockSpec((rows, slots), lambda h: (0, 0)),
        ]
    shape = jax.ShapeDtypeStruct((rows, features), jnp.float32)
    out_spec = pl.BlockSpec((rows, block), lambda h: (0, h))
    return pl.pallas_call(
        functools.partial(attend_kernel, count=len(sources), scale=1.0 / math.sqrt(HD)),
        grid=(pairs,),
        in_specs=specs,
        out_specs=(out_spec, out_spec, out_spec),
        out_shape=(shape, shape, shape),
    )(*operands)


def dp_ring(mesh):
    count = mesh.shape["dp"]
    try:
        axis = list(mesh.axis_names).index("dp")
        places = [tuple(mesh.devices.take(i, axis=axis).reshape(-1)[0].coords) for i in range(count)]
        varying = [a for a in range(len(places[0])) if len({c[a] for c in places}) > 1]
        changes = {a: sum(places[i][a] != places[i + 1][a] for i in range(count - 1)) for a in varying}
        slow, fast = sorted(varying, key=lambda a: changes[a])
        rows = sorted({c[slow] for c in places})
        cols = sorted({c[fast] for c in places})
        where = {(c[slow], c[fast]): i for i, c in enumerate(places)}
        if len(varying) != 2 or len(rows) * len(cols) != count or len(rows) % 2 or len(cols) < 2:
            raise ValueError
        cycle = [where[(rows[0], cols[0])]]
        for r, row in enumerate(rows):
            ordered = cols[1:] if r % 2 == 0 else cols[1:][::-1]
            cycle += [where[(row, col)] for col in ordered]
        cycle += [where[(row, cols[0])] for row in rows[1:][::-1]]
        if sorted(cycle) != list(range(count)):
            raise ValueError
        return cycle
    except Exception:
        return list(range(count))


def ring_gather(piece, ring, step):
    count = len(ring)
    pairs = [(ring[p], ring[(p + step) % count]) for p in range(count)]
    arrived = [piece]
    for unused in range(count - 1):
        piece = lax.ppermute(piece, "dp", pairs)
        arrived.append(piece)
    return arrived


def ring_reduce(blocks, ring, step):
    count = len(ring)
    pairs = [(ring[p], ring[(p + step) % count]) for p in range(count)]
    moving = blocks[1]
    for index in range(2, count):
        received = lax.ppermute(moving, "dp", pairs).astype(jnp.float32)
        moving = (received + blocks[index].astype(jnp.float32)).astype(jnp.bfloat16)
    received = lax.ppermute(moving, "dp", pairs).astype(jnp.float32)
    return received + blocks[0].astype(jnp.float32)


def local(
    ring,
    expert_count,
    hidden,
    tree_qkv,
    prompt_kv,
    prompt_len,
    private_kv,
    priv_len,
    parents,
    leaf,
    w_out,
    norm_gain,
    w_router,
    routes,
    w_gate_up,
    w_down,
):
    row_count = hidden.shape[0]
    features = hidden.shape[1]
    new_kv = tree_qkv[:, features:]
    reached = closure(parents)
    grouped_kv = new_kv.reshape(REQ_DEV, TREE, 2 * features)
    blocks = features // ((4 if (features // HD) % 4 == 0 else 2) * HD)
    private_slots = jnp.arange(private_kv.shape[1], dtype=jnp.int32)
    private_ok = jnp.broadcast_to(private_slots[None, :] < priv_len[0], (row_count, private_kv.shape[1]))
    piece = prompt_kv[0]
    piece_len = piece.shape[0]
    own = lax.axis_index("expert")
    places = jnp.arange(piece_len, dtype=jnp.int32)

    def prompt_ok(source):
        return jnp.broadcast_to((source * piece_len + places < prompt_len[0])[None, :], (row_count, piece_len))

    local_sources = [
        (private_kv[0], 0, blocks, private_ok),
        (tree_qkv, blocks, 2 * blocks, reached[0] > 0.5),
    ]
    if expert_count == 4:
        def swap(rows, mask):
            return lax.ppermute(rows, "expert", [(j, j ^ mask) for j in range(expert_count)])

        near = swap(piece, 1)
        far = swap(piece, 2)
        corner = swap(far, 1)
        local_sources.append((piece, 0, blocks, prompt_ok(own)))
        remote_sources = [
            (near, 0, blocks, prompt_ok(own ^ 1)),
            (far, 0, blocks, prompt_ok(own ^ 2)),
            (corner, 0, blocks, prompt_ok(own ^ 3)),
        ]
    else:
        gathered = lax.all_gather(prompt_kv, "expert", axis=1, tiled=True)[0]
        whole = jnp.arange(gathered.shape[0], dtype=jnp.int32)
        remote_sources = [
            (gathered, 0, blocks, jnp.broadcast_to((whole < prompt_len[0])[None, :], (row_count, gathered.shape[0])))
        ]
    local_acc, local_top, local_total = attend(tree_qkv[:, :features], local_sources)
    prompt_acc, prompt_top, prompt_total = attend(tree_qkv[:, :features], remote_sources)
    highest = jnp.maximum(local_top, prompt_top)
    scale_local = jnp.exp(local_top - highest)
    scale_prompt = jnp.exp(prompt_top - highest)
    totals = local_total * scale_local + prompt_total * scale_prompt
    weighted = local_acc * scale_local + prompt_acc * scale_prompt
    context = (weighted / totals).astype(jnp.bfloat16)
    attended = jnp.dot(context, w_out, preferred_element_type=jnp.float32)
    middle = (hidden.astype(jnp.float32) + attended).astype(jnp.bfloat16)
    middle32 = middle.astype(jnp.float32)
    normed = (
        middle32 * lax.rsqrt(jnp.mean(middle32 * middle32, axis=1, keepdims=True) + EPS) * norm_gain
    ).astype(jnp.bfloat16)
    logits = jnp.dot(normed, w_router, preferred_element_type=jnp.float32)
    experts = w_router.shape[1]
    choose = routes[:, :, None] == jnp.arange(experts, dtype=jnp.int32)[None, None, :]
    picked = jnp.sum(jnp.where(choose, logits[:, None, :], 0.0), axis=2)
    gate_first = jax.nn.sigmoid(picked[:, 0] - picked[:, 1])
    gate_second = jax.nn.sigmoid(picked[:, 1] - picked[:, 0])
    capacity = 3 * row_count // experts
    onehot = choose.reshape(2 * row_count, experts).astype(jnp.float32)
    assign_ids = jnp.arange(2 * row_count, dtype=jnp.int32)
    earlier = (assign_ids[None, :] < assign_ids[:, None]).astype(jnp.float32)
    before = jnp.dot(earlier, onehot, precision=HIGH)
    slot_rank = jnp.sum(before * onehot, axis=1).astype(jnp.int32)
    own = lax.axis_index("expert")
    shift_of = (routes.reshape(2 * row_count) - own) % experts
    target = shift_of * capacity + slot_rank
    select = (jnp.arange(experts * capacity, dtype=jnp.int32)[:, None] == target[None, :]).astype(
        jnp.bfloat16
    )
    doubled = jnp.repeat(normed, 2, axis=0)
    outgoing = (
        jnp.dot(select, doubled, preferred_element_type=jnp.float32)
        .astype(jnp.bfloat16)
        .reshape(experts, capacity, features)
    )
    gate_cols = w_gate_up[0, 0]
    up_cols = w_gate_up[0, 1]
    down_rows = w_down[0]
    def shifted(rows, shift):
        if shift % experts == 0:
            return rows
        return lax.ppermute(rows, "expert", [(j, (j + shift) % experts) for j in range(experts)])

    arrived = [shifted(outgoing[shift], shift) for shift in range(experts)]
    half = experts * capacity // 2
    forward = ring_gather(jnp.concatenate(arrived[: experts // 2], axis=0), ring, 1)
    backward = ring_gather(jnp.concatenate(arrived[experts // 2 :], axis=0), ring, -1)
    forward_out = []
    backward_out = []
    for index in range(len(ring)):
        pooled = jnp.concatenate([forward[index], backward[index]], axis=0)
        gate_act = jnp.dot(pooled, gate_cols, preferred_element_type=jnp.float32)
        upper = jnp.dot(pooled, up_cols, preferred_element_type=jnp.float32)
        hidden_units = (jax.nn.silu(gate_act) * upper).astype(jnp.bfloat16)
        partial = jnp.dot(hidden_units, down_rows, preferred_element_type=jnp.float32).astype(jnp.bfloat16)
        forward_out.append(partial[:half])
        backward_out.append(partial[half:])
    summed_rows = jnp.concatenate(
        [ring_reduce(forward_out, ring, 1), ring_reduce(backward_out, ring, -1)], axis=0
    ).astype(jnp.bfloat16).reshape(experts, capacity, features)
    flat_back = jnp.concatenate(
        [shifted(summed_rows[shift], -shift) for shift in range(experts)], axis=0
    )
    pick = (target[:, None] == jnp.arange(experts * capacity, dtype=jnp.int32)[None, :]).astype(jnp.bfloat16)
    fetched = jnp.dot(pick, flat_back, preferred_element_type=jnp.float32).reshape(row_count, 2, features)
    layer_out = (
        middle32 + gate_first[:, None] * fetched[:, 0] + gate_second[:, None] * fetched[:, 1]
    ).astype(jnp.bfloat16)
    accepted_kv = jax.vmap(compact)(reached, leaf, grouped_kv)
    return (layer_out, accepted_kv)


def solution(mesh):
    placed = (
        P(("dp", "expert"), None),
        P(("dp", "expert"), None),
        P("dp", "expert", None),
        P("dp"),
        P(("dp", "expert"), None, None),
        P(("dp", "expert")),
        P(("dp", "expert"), None),
        P(("dp", "expert")),
        P(),
        P(),
        P(),
        P(("dp", "expert"), None),
        P("expert", None, None, "dp"),
        P("expert", "dp", None),
    )
    ring = dp_ring(mesh)
    return jax.shard_map(
        functools.partial(local, ring, mesh.shape["expert"]),
        mesh=mesh,
        in_specs=placed,
        out_specs=(P(("dp", "expert"), None), P(("dp", "expert"), None, None)),
        check_vma=False,
    )
```
